512 devices in a mesh: chain: 32 (over z, core), src: 16 (over y, x).
Axes of the slice: x: 4, y: 4, z: 16, core: 2. Of those that a mesh axis runs over, the one named last changes fastest.
Arguments:
- sources: bfloat16 [1024, 16384], P('src', 'chain'), may hold values from -6 to 6
- forward: bfloat16 [1024, 16384], P('src', 'chain')
- inv_diag: bfloat16 [32, 512, 512], P('chain'), as said below
- coupling: bfloat16 [32, 2, 512, 512], P('chain'), may hold values from -0.5 to 0.5
- pattern: int32 [32, 2], P('chain'), may hold values 0 or 1
Outputs:
- adjoint: bfloat16 [1024, 16384], P('src', 'chain')
- direction: float32 [16384], P('chain')
The draws below stay inside these ranges and needn't reach their ends.
Inputs may be any that keep to these rules, and one draw needn't show every extreme that they name: inv_diag is the identity plus a dense perturbation of spectral size about one.
All inputs are finite; a program needn't handle non-finite values. No bound on the sum of `pattern` on one device may be relied on, other than what follows from the above.
Results may differ from the reference program's by a relative error of at most 0.02.
Values may be sent and summed in bfloat16 or wider, within the bound.
No kernel may reach another device: no remote copies, remote signals or barrier semaphores. Data moves between devices by JAX's collectives and lax.ppermute only.
A program may use at most 64 MiB of HBM per device.

```python
import jax
import jax.numpy as jnp
from jax import lax

B = 512
SRC_DEV = 64
NP = 32
NCELL = 16384
TOTAL_SRC = 1024


def draw_inv_diag(key, part):
    spread = jax.random.normal(key, (NP, B, B), jnp.float32)
    spread = jnp.clip(spread, -6.0, 6.0) * (0.5 / B ** 0.5)
    return (jnp.eye(B, dtype=jnp.float32)[None] + spread).astype(jnp.bfloat16)


def draw_forward(key, part):
    key_values, key_cols = jax.random.split(key, 2)
    groups = TOTAL_SRC // SRC_DEV
    group_index = jnp.arange(TOTAL_SRC, dtype=jnp.float32)[:, None] // SRC_DEV
    row_scale = 3.0 ** (group_index / max(groups - 1, 1)) * 0.5
    col_scale = 10.0 ** jax.random.uniform(key_cols, (1, NCELL), jnp.float32, -0.5, 0.5)
    values = jnp.clip(jax.random.normal(key_values, (TOTAL_SRC, NCELL), jnp.float32), -4.0, 4.0)
    return (values * row_scale * col_scale).astype(jnp.bfloat16)


def set_ends(entries, key, smallest, high):
    longest = entries.shape.index(max(entries.shape))
    spots = []
    for shift in (0, 1):
        where = [jax.random.randint(jax.random.fold_in(key, axis), (), 0, length) for axis, length in enumerate(entries.shape)]
        where[longest] = (where[longest] + shift) % entries.shape[longest]
        spots.append(tuple(where))
    return entries.at[spots[0]].set(smallest).at[spots[1]].set(high)


def steps_of(rng, shape, cuts, smallest, high):
    factor_of = 1.0
    for axis_at, blocks in cuts:
        steps = jax.random.uniform(jax.random.fold_in(jax.random.fold_in(rng, 6), axis_at), (blocks,), jnp.float32, smallest / len(cuts), high / len(cuts))
        factor_of = factor_of * jnp.repeat(jnp.exp(steps), shape[axis_at] // blocks).reshape((-1,) + (1,) * (len(shape) - 1 - axis_at))
    return factor_of


def centred(rng, dims, scale, bound, cuts=(), held_as=jnp.bfloat16):
    gain = steps_of(rng, dims, cuts, -0.22, 0.18) if cuts else 1.0
    result = jax.random.normal(rng, dims, jnp.float32) * scale * gain
    return jnp.minimum(jnp.maximum(result, -bound), bound).astype(held_as)


def setup_inputs(seed: int = 0) -> dict:
    splits = jax.random.split(jax.random.key(seed), 6)
    return {
        "sources": centred(splits[0], (TOTAL_SRC, NCELL), 1.0, 6.0, ((0, 16), (1, 32))),
        "forward": draw_forward(jax.random.fold_in(splits[5], 71), 0),
        "inv_diag": draw_inv_diag(jax.random.fold_in(splits[5], 71), 0),
        "coupling": centred(splits[3], (NP, 2, B, B), (0.75 / B ** 0.5), 0.5, ((0, 32),)),
        "pattern": set_ends((jax.random.randint(splits[4], (NP, 2), 0, 3) < 2).astype(jnp.int32), jax.random.fold_in(splits[4], 1), 0, 1),
    }


def reference(sources, forward, inv_diag, coupling, pattern):
    empty = jnp.zeros((TOTAL_SRC, B), jnp.bfloat16)
    solved = [empty for panel in range(NP + 2)]
    for panel in reversed(range(NP)):
        rows = sources[:, panel * B:(panel + 1) * B].astype(jnp.float32)
        first = jnp.dot(solved[panel + 1], coupling[panel, 0], preferred_element_type=jnp.float32)
        second = jnp.dot(solved[panel + 2], coupling[panel, 1], preferred_element_type=jnp.float32)
        rows = rows - pattern[panel, 0].astype(jnp.float32) * first - pattern[panel, 1].astype(jnp.float32) * second
        solved[panel] = jnp.dot(rows.astype(jnp.bfloat16), inv_diag[panel], preferred_element_type=jnp.float32).astype(jnp.bfloat16)
    adjoint = jnp.concatenate(solved[:NP], axis=1)
    grad = lax.optimization_barrier(jnp.sum(forward.astype(jnp.float32) * adjoint.astype(jnp.float32), axis=0))
    scale = jnp.sqrt(jnp.mean(grad * grad) + 1e-06)
    return (adjoint, grad / scale)
```

```python
import jax
import jax.numpy as jnp
from jax import lax
from jax.sharding import PartitionSpec as P


def shifted(x, axis, by):
    devices = lax.axis_size(axis)
    pairs = [(i, i + by) for i in range(devices) if 0 <= i + by < devices]
    return lax.ppermute(x, axis, pairs)


def swapped(x, axis, bit):
    devices = lax.axis_size(axis)
    return lax.ppermute(x, axis, [(i, i ^ bit) for i in range(devices)])


def butterfly_sum(x, axis):
    devices = lax.axis_size(axis)
    bit = 1
    while bit < devices:
        x = x + swapped(x, axis, bit)
        bit *= 2
    return x


def solve_panel(rows, nearer, farther, inv_block, coupled):
    both = jnp.concatenate([nearer, farther], axis=1)
    total = rows.astype(jnp.float32) - jnp.dot(
        both, coupled, preferred_element_type=jnp.float32
    )
    return jnp.dot(
        total.astype(jnp.bfloat16), inv_block, preferred_element_type=jnp.float32
    ).astype(jnp.bfloat16)


def per_device(sources, forward, inv_diag, coupling, pattern):
    chain_size = lax.axis_size("chain")
    chips = chain_size // 2
    core = lax.axis_index("chain") % 2
    is_low = core == 0
    src_rows = sources.shape[0]
    half = src_rows // 2
    width = sources.shape[1]

    weights = pattern[0].astype(coupling.dtype)
    coupled = jnp.concatenate(
        [coupling[0, 0] * weights[0], coupling[0, 1] * weights[1]], axis=0
    )
    inv_block = inv_diag[0]

    mine = lax.dynamic_slice_in_dim(sources, core * half, half, axis=0)
    given = lax.dynamic_slice_in_dim(sources, (1 - core) * half, half, axis=0)
    other_coupled, other_inv, other_rows = swapped(
        (coupled, inv_block, given), "chain", 1
    )
    high_coupled = jnp.where(is_low, other_coupled, coupled)
    high_inv = jnp.where(is_low, other_inv, inv_block)
    high_rows = jnp.where(is_low, other_rows, mine)
    low_coupled = jnp.where(is_low, coupled, other_coupled)
    low_inv = jnp.where(is_low, inv_block, other_inv)
    low_rows = jnp.where(is_low, mine, other_rows)

    def both_panels(nearer, farther):
        high = solve_panel(high_rows, nearer, farther, high_inv, high_coupled)
        low = solve_panel(low_rows, high, nearer, low_inv, low_coupled)
        return low, high

    def sweep(step, carry):
        nearer, farther = carry
        low, high = both_panels(nearer, farther)
        packed = shifted(jnp.concatenate([low, high], axis=0), "chain", -2)
        return packed[:half], packed[half:]

    zeros_rows = jnp.zeros((half, width), jnp.bfloat16)
    nearer, farther = lax.fori_loop(0, chips - 1, sweep, (zeros_rows, zeros_rows))
    low, high = both_panels(nearer, farther)

    back = swapped(jnp.where(is_low, high, low), "chain", 1)
    adjoint = jnp.where(
        is_low,
        jnp.concatenate([low, back], axis=0),
        jnp.concatenate([back, high], axis=0),
    )

    partial_image = jnp.sum(forward.astype(jnp.float32) * adjoint.astype(jnp.float32), axis=0)
    count = float(chain_size * width)
    grad = butterfly_sum(partial_image, "src")
    squares = butterfly_sum(jnp.sum(grad * grad), "chain")
    direction = grad / jnp.sqrt(squares / count + 1e-06)
    return (adjoint, direction)


def solution(mesh):
    return jax.shard_map(
        per_device,
        mesh=mesh,
        in_specs=(
            P("src", "chain"),
            P("src", "chain"),
            P("chain", None, None),
            P("chain", None, None, None),
            P("chain", None),
        ),
        out_specs=(P("src", "chain"), P("chain")),
        check_vma=False,
    )
```

```python
import jax
import jax.numpy as jnp
from jax import lax
from jax.sharding import PartitionSpec as P


def shifted(x, axis, by):
    devices = lax.axis_size(axis)
    pairs = [(i, i + by) for i in range(devices) if 0 <= i + by < devices]
    return lax.ppermute(x, axis, pairs)


def swapped(x, axis, bit):
    devices = lax.axis_size(axis)
    return lax.ppermute(x, axis, [(i, i ^ bit) for i in range(devices)])


def gathered_sum(x, axes, members, position):
    size = len(members[0])
    received = [x]
    for step in range(1, size):
        pairs = []
        for group in members:
            for g, device in enumerate(group):
                pairs.append((group[(g + step) % size], device))
        received.append(lax.ppermute(x, axes, pairs))
    stacked = jnp.roll(jnp.stack(received), position, axis=0)
    return jnp.sum(stacked, axis=0)


def solve_panel(rows, nearer, farther, inv_block, coupled, weights):
    both = jnp.concatenate([nearer * weights[0], farther * weights[1]], axis=1)
    total = rows.astype(jnp.float32) - jnp.dot(
        both, coupled, preferred_element_type=jnp.float32
    )
    return jnp.dot(
        total.astype(jnp.bfloat16), inv_block, preferred_element_type=jnp.float32
    ).astype(jnp.bfloat16)


def per_device(sources, forward, inv_diag, coupling, pattern):
    chain_size = lax.axis_size("chain")
    src_size = lax.axis_size("src")
    chips = chain_size // 2
    chain_index = lax.axis_index("chain")
    src_index = lax.axis_index("src")
    core = chain_index % 2
    chip = chain_index // 2
    is_low = core == 0
    src_rows = sources.shape[0]
    half = src_rows // 2
    width = sources.shape[1]

    weights = pattern[0].astype(jnp.bfloat16)
    coupled = coupling[0].reshape(2 * width, width)
    inv_block = inv_diag[0]

    mine = lax.dynamic_slice_in_dim(sources, core * half, half, axis=0)
    given = lax.dynamic_slice_in_dim(sources, (1 - core) * half, half, axis=0)
    mine_fwd = lax.dynamic_slice_in_dim(forward, core * half, half, axis=0)
    given_fwd = lax.dynamic_slice_in_dim(forward, (1 - core) * half, half, axis=0)
    other_coupled, other_inv, other_rows, other_fwd, other_weights = swapped(
        (coupled, inv_block, given, given_fwd, weights), "chain", 1
    )
    high_coupled = jnp.where(is_low, other_coupled, coupled)
    high_inv = jnp.where(is_low, other_inv, inv_block)
    high_rows = jnp.where(is_low, other_rows, mine)
    high_weights = jnp.where(is_low, other_weights, weights)
    low_coupled = jnp.where(is_low, coupled, other_coupled)
    low_inv = jnp.where(is_low, inv_block, other_inv)
    low_rows = jnp.where(is_low, mine, other_rows)
    low_weights = jnp.where(is_low, weights, other_weights)
    high_fwd = jnp.where(is_low, other_fwd, mine_fwd)
    low_fwd = jnp.where(is_low, mine_fwd, other_fwd)

    def both_panels(nearer, farther):
        high = solve_panel(high_rows, nearer, farther, high_inv, high_coupled, high_weights)
        low = solve_panel(low_rows, high, nearer, low_inv, low_coupled, low_weights)
        return low, high

    def sweep(step, carry):
        nearer, farther = carry
        low, high = both_panels(nearer, farther)
        packed = shifted(jnp.concatenate([low, high], axis=0), "chain", -2)
        return packed[:half], packed[half:]

    zeros_rows = jnp.zeros((half, width), jnp.bfloat16)
    nearer, farther = lax.fori_loop(0, chips - 1, sweep, (zeros_rows, zeros_rows))
    low, high = both_panels(nearer, farther)

    back = swapped(jnp.where(is_low, high, low), "chain", 1)
    adjoint = jnp.where(
        is_low,
        jnp.concatenate([low, back], axis=0),
        jnp.concatenate([back, high], axis=0),
    )

    partial_image = jnp.concatenate(
        [
            jnp.sum(low_fwd.astype(jnp.float32) * low.astype(jnp.float32), axis=0),
            jnp.sum(high_fwd.astype(jnp.float32) * high.astype(jnp.float32), axis=0),
        ]
    )
    plane = [
        [(2 * z + c) * src_size + s for c in range(2) for s in range(src_size)]
        for z in range(chips)
    ]
    grad = gathered_sum(partial_image, ("chain", "src"), plane, core * src_size + src_index)
    chip_squares = jnp.sum(grad * grad)
    line = [[2 * z + c for z in range(chips)] for c in range(2)]
    squares = gathered_sum(chip_squares, "chain", line, chip)
    count = float(chain_size * width)
    scale = jnp.sqrt(squares / count + 1e-06)
    direction = jnp.where(is_low, grad[:width], grad[width:]) / scale
    return (adjoint, direction)


def solution(mesh):
    return jax.shard_map(
        per_device,
        mesh=mesh,
        in_specs=(
            P("src", "chain"),
            P("src", "chain"),
            P("chain", None, None),
            P("chain", None, None, None),
            P("chain", None),
        ),
        out_specs=(P("src", "chain"), P("chain")),
        check_vma=False,
    )
```

```python
import jax
import jax.numpy as jnp
from jax import lax
from jax.sharding import Mesh
from jax.sharding import PartitionSpec as P

CHAIN = ("chip", "core")


def shifted(x, axis, by):
    devices = lax.axis_size(axis)
    pairs = [(i, i + by) for i in range(devices) if 0 <= i + by < devices]
    return lax.ppermute(x, axis, pairs)


def swapped(x, axis):
    return lax.ppermute(x, axis, [(0, 1), (1, 0)])


def summed_over(x, axes):
    members = 1
    for axis in axes:
        members *= lax.axis_size(axis)
    spread = jnp.broadcast_to(x, (members,) + x.shape)
    return jnp.sum(lax.all_to_all(spread, axes, 0, 0, tiled=True), axis=0)


def solve_panel(rows, nearer, farther, inv_block, coupled):
    both = jnp.concatenate([nearer, farther], axis=1)
    total = rows.astype(jnp.float32) - jnp.dot(
        both, coupled, preferred_element_type=jnp.float32
    )
    return jnp.dot(
        total.astype(jnp.bfloat16), inv_block, preferred_element_type=jnp.float32
    ).astype(jnp.bfloat16)


def per_device(sources, forward, inv_diag, coupling, pattern):
    chips = lax.axis_size("chip")
    core = lax.axis_index("core")
    is_low = core == 0
    src_rows = sources.shape[0]
    half = src_rows // 2
    width = sources.shape[1]

    weights = pattern[0].astype(coupling.dtype)
    coupled = jnp.concatenate(
        [coupling[0, 0] * weights[0], coupling[0, 1] * weights[1]], axis=0
    )
    inv_block = inv_diag[0]

    mine = lax.dynamic_slice_in_dim(sources, core * half, half, axis=0)
    given = lax.dynamic_slice_in_dim(sources, (1 - core) * half, half, axis=0)
    mine_fwd = lax.dynamic_slice_in_dim(forward, core * half, half, axis=0)
    given_fwd = lax.dynamic_slice_in_dim(forward, (1 - core) * half, half, axis=0)
    other_coupled, other_inv, other_rows, other_fwd = swapped(
        (coupled, inv_block, given, given_fwd), "core"
    )
    high_coupled = jnp.where(is_low, other_coupled, coupled)
    high_inv = jnp.where(is_low, other_inv, inv_block)
    high_rows = jnp.where(is_low, other_rows, mine)
    low_coupled = jnp.where(is_low, coupled, other_coupled)
    low_inv = jnp.where(is_low, inv_block, other_inv)
    low_rows = jnp.where(is_low, mine, other_rows)

    def both_panels(nearer, farther):
        high = solve_panel(high_rows, nearer, farther, high_inv, high_coupled)
        low = solve_panel(low_rows, high, nearer, low_inv, low_coupled)
        return low, high

    def sweep(step, carry):
        nearer, farther = carry
        low, high = both_panels(nearer, farther)
        packed = shifted(jnp.concatenate([low, high], axis=0), "chip", -1)
        return packed[:half], packed[half:]

    zeros_rows = jnp.zeros((half, width), jnp.bfloat16)
    nearer, farther = lax.fori_loop(0, chips - 1, sweep, (zeros_rows, zeros_rows))
    low, high = both_panels(nearer, farther)

    back = swapped(jnp.where(is_low, high, low), "core")
    adjoint = jnp.where(
        is_low,
        jnp.concatenate([low, back], axis=0),
        jnp.concatenate([back, high], axis=0),
    )

    high_fwd = jnp.where(is_low, other_fwd, mine_fwd)
    low_fwd = jnp.where(is_low, mine_fwd, other_fwd)
    partial_image = jnp.concatenate(
        [
            jnp.sum(low_fwd.astype(jnp.float32) * low.astype(jnp.float32), axis=0),
            jnp.sum(high_fwd.astype(jnp.float32) * high.astype(jnp.float32), axis=0),
        ]
    )
    grad = summed_over(partial_image, ("core", "src"))
    squares = summed_over(jnp.sum(grad * grad), ("chip",))
    count = float(chips * 2 * width)
    scale = jnp.sqrt(squares / count + 1e-06)
    direction = jnp.where(is_low, grad[:width], grad[width:]) / scale
    return (adjoint, direction)


def solution(mesh):
    chain = mesh.shape["chain"]
    src = mesh.shape["src"]
    devices = mesh.devices
    if mesh.axis_names != ("chain", "src"):
        devices = devices.T
    split = Mesh(devices.reshape(chain // 2, 2, src), ("chip", "core", "src"))
    return jax.shard_map(
        per_device,
        mesh=split,
        in_specs=(
            P("src", CHAIN),
            P("src", CHAIN),
            P(CHAIN, None, None),
            P(CHAIN, None, None, None),
            P(CHAIN, None),
        ),
        out_specs=(P("src", CHAIN), P(CHAIN)),
        check_vma=False,
    )
```

```python
import jax
import jax.numpy as jnp
from jax import lax
from jax.sharding import Mesh
from jax.sharding import PartitionSpec as P

CHAIN = ("chip", "core")


def shifted(x, axis, by):
    devices = lax.axis_size(axis)
    pairs = [(i, i + by) for i in range(devices) if 0 <= i + by < devices]
    return lax.ppermute(x, axis, pairs)


def swapped(x, axis):
    return lax.ppermute(x, axis, [(0, 1), (1, 0)])


def summed_over(x, axes):
    members = 1
    for axis in axes:
        members *= lax.axis_size(axis)
    spread = jnp.broadcast_to(x, (members,) + x.shape)
    return jnp.sum(lax.all_to_all(spread, axes, 0, 0, tiled=True), axis=0)


def spread_sum(chip_value, chips, src_size):
    pairs = [
        (z * src_size + s, ((z + s) % chips) * src_size + s)
        for z in range(chips)
        for s in range(1, chips)
    ]
    moved = lax.ppermute(chip_value, ("chip", "src"), pairs)
    src_index = lax.axis_index("src")
    moved = jnp.where(src_index == 0, chip_value, moved)
    moved = jnp.where(src_index < chips, moved, 0.0)
    return summed_over(moved, ("src",))


def solve_panel(rows, nearer, farther, inv_block, coupled):
    both = jnp.concatenate([nearer, farther], axis=1)
    total = rows.astype(jnp.float32) - jnp.dot(
        both, coupled, preferred_element_type=jnp.float32
    )
    return jnp.dot(
        total.astype(jnp.bfloat16), inv_block, preferred_element_type=jnp.float32
    ).astype(jnp.bfloat16)


def per_device(sources, forward, inv_diag, coupling, pattern):
    chips = lax.axis_size("chip")
    core = lax.axis_index("core")
    is_low = core == 0
    src_rows = sources.shape[0]
    half = src_rows // 2
    width = sources.shape[1]

    weights = pattern[0].astype(coupling.dtype)
    inv_block = inv_diag[0]

    mine = lax.dynamic_slice_in_dim(sources, core * half, half, axis=0)
    given = lax.dynamic_slice_in_dim(sources, (1 - core) * half, half, axis=0)
    mine_fwd = lax.dynamic_slice_in_dim(forward, core * half, half, axis=0)
    given_fwd = lax.dynamic_slice_in_dim(forward, (1 - core) * half, half, axis=0)
    packed = jnp.concatenate(
        [
            coupling[0, 0] * weights[0],
            coupling[0, 1] * weights[1],
            inv_block,
            given,
            given_fwd,
        ],
        axis=0,
    )
    coupled = packed[: 2 * width]
    other = swapped(packed, "core")
    other_coupled = other[: 2 * width]
    other_inv = other[2 * width : 3 * width]
    other_rows = other[3 * width : 3 * width + half]
    other_fwd = other[3 * width + half :]
    high_coupled = jnp.where(is_low, other_coupled, coupled)
    high_inv = jnp.where(is_low, other_inv, inv_block)
    high_rows = jnp.where(is_low, other_rows, mine)
    low_coupled = jnp.where(is_low, coupled, other_coupled)
    low_inv = jnp.where(is_low, inv_block, other_inv)
    low_rows = jnp.where(is_low, mine, other_rows)

    def both_panels(nearer, farther):
        high = solve_panel(high_rows, nearer, farther, high_inv, high_coupled)
        low = solve_panel(low_rows, high, nearer, low_inv, low_coupled)
        return low, high

    def sweep(step, carry):
        nearer, farther = carry
        low, high = both_panels(nearer, farther)
        packed = shifted(jnp.concatenate([low, high], axis=0), "chip", -1)
        return packed[:half], packed[half:]

    zeros_rows = jnp.zeros((half, width), jnp.bfloat16)
    nearer, farther = lax.fori_loop(0, chips - 1, sweep, (zeros_rows, zeros_rows))
    low, high = both_panels(nearer, farther)

    back = swapped(jnp.where(is_low, high, low), "core")
    adjoint = jnp.where(
        is_low,
        jnp.concatenate([low, back], axis=0),
        jnp.concatenate([back, high], axis=0),
    )

    high_fwd = jnp.where(is_low, other_fwd, mine_fwd)
    low_fwd = jnp.where(is_low, mine_fwd, other_fwd)
    partial_image = jnp.concatenate(
        [
            jnp.sum(low_fwd.astype(jnp.float32) * low.astype(jnp.float32), axis=0),
            jnp.sum(high_fwd.astype(jnp.float32) * high.astype(jnp.float32), axis=0),
        ]
    )
    grad = summed_over(partial_image, ("core", "src"))
    chip_squares = jnp.sum(grad * grad)
    src_size = lax.axis_size("src")
    if src_size < chips:
        squares = summed_over(chip_squares, ("chip",))
    else:
        squares = spread_sum(chip_squares, chips, src_size)
    count = float(chips * 2 * width)
    count = float(chips * 2 * width)
    scale = jnp.sqrt(squares / count + 1e-06)
    direction = jnp.where(is_low, grad[:width], grad[width:]) / scale
    return (adjoint, direction)


def solution(mesh):
    chain = mesh.shape["chain"]
    src = mesh.shape["src"]
    devices = mesh.devices
    if mesh.axis_names != ("chain", "src"):
        devices = devices.T
    split = Mesh(devices.reshape(chain // 2, 2, src), ("chip", "core", "src"))
    return jax.shard_map(
        per_device,
        mesh=split,
        in_specs=(
            P("src", CHAIN),
            P("src", CHAIN),
            P(CHAIN, None, None),
            P(CHAIN, None, None, None),
            P(CHAIN, None),
        ),
        out_specs=(P("src", CHAIN), P(CHAIN)),
        check_vma=False,
    )
```

```python
import jax
import jax.numpy as jnp
from jax import lax
from jax.sharding import Mesh
from jax.sharding import PartitionSpec as P

CHAIN = ("chip", "core")


def shifted(x, axis, by):
    devices = lax.axis_size(axis)
    pairs = [(i, i + by) for i in range(devices) if 0 <= i + by < devices]
    return lax.ppermute(x, axis, pairs)


def swapped(x, axis):
    return lax.ppermute(x, axis, [(0, 1), (1, 0)])


def summed_over(x, axes):
    members = 1
    for axis in axes:
        members *= lax.axis_size(axis)
    spread = jnp.broadcast_to(x, (members,) + x.shape)
    return jnp.sum(lax.all_to_all(spread, axes, 0, 0, tiled=True), axis=0)


def solve_panel(rows, nearer, farther, inv_block, coupled):
    both = jnp.concatenate([nearer, farther], axis=1)
    total = rows.astype(jnp.float32) - jnp.dot(
        both, coupled, preferred_element_type=jnp.float32
    )
    return jnp.dot(
        total.astype(jnp.bfloat16), inv_block, preferred_element_type=jnp.float32
    ).astype(jnp.bfloat16)


def per_device(sources, forward, inv_diag, coupling, pattern):
    chips = lax.axis_size("chip")
    core = lax.axis_index("core")
    is_low = core == 0
    width = sources.shape[1]

    weights = pattern[0].astype(coupling.dtype)
    coupled = jnp.concatenate(
        [coupling[0, 0] * weights[0], coupling[0, 1] * weights[1]], axis=0
    )
    inv_block = inv_diag[0]

    other_coupled, other_inv, other_rows, other_fwd = swapped(
        (coupled, inv_block, sources, forward), "core"
    )

    def both_panels(nearer, farther):
        high = solve_panel(sources, nearer, farther, inv_block, coupled)
        low = solve_panel(other_rows, high, nearer, other_inv, other_coupled)
        return low, high

    carriers = [(2 * z + 1, 2 * z - 1) for z in range(1, chips)]

    def sweep(step, carry):
        nearer, farther = carry
        low, high = both_panels(nearer, farther)
        packed = lax.ppermute(
            jnp.concatenate([low, high], axis=0), CHAIN, carriers
        )
        return packed[: sources.shape[0]], packed[sources.shape[0] :]

    zeros_rows = jnp.zeros(sources.shape, jnp.bfloat16)
    nearer, farther = lax.fori_loop(0, chips - 1, sweep, (zeros_rows, zeros_rows))
    low, high = both_panels(nearer, farther)

    given = lax.ppermute(low, "core", [(1, 0)])
    adjoint = jnp.where(is_low, given, high)

    partial_image = jnp.concatenate(
        [
            jnp.sum(other_fwd.astype(jnp.float32) * low.astype(jnp.float32), axis=0),
            jnp.sum(forward.astype(jnp.float32) * high.astype(jnp.float32), axis=0),
        ]
    )
    partial_image = jnp.where(is_low, 0.0, partial_image)
    grad = summed_over(partial_image, ("core", "src"))
    squares = summed_over(jnp.sum(grad * grad), ("chip",))
    count = float(chips * 2 * width)
    scale = jnp.sqrt(squares / count + 1e-06)
    direction = jnp.where(is_low, grad[:width], grad[width:]) / scale
    return (adjoint, direction)


def solution(mesh):
    chain = mesh.shape["chain"]
    src = mesh.shape["src"]
    devices = mesh.devices
    if mesh.axis_names != ("chain", "src"):
        devices = devices.T
    split = Mesh(devices.reshape(chain // 2, 2, src), ("chip", "core", "src"))
    return jax.shard_map(
        per_device,
        mesh=split,
        in_specs=(
            P("src", CHAIN),
            P("src", CHAIN),
            P(CHAIN, None, None),
            P(CHAIN, None, None, None),
            P(CHAIN, None),
        ),
        out_specs=(P("src", CHAIN), P(CHAIN)),
        check_vma=False,
    )
```

```python
import jax
import jax.numpy as jnp
from jax import lax
from jax.sharding import Mesh
from jax.sharding import PartitionSpec as P

CHAIN = ("chip", "core")


def shifted(x, axis, by):
    devices = lax.axis_size(axis)
    pairs = [(i, i + by) for i in range(devices) if 0 <= i + by < devices]
    return lax.ppermute(x, axis, pairs)


def swapped(x, axis):
    return lax.ppermute(x, axis, [(0, 1), (1, 0)])


def summed_over(x, axes):
    members = 1
    for axis in axes:
        members *= lax.axis_size(axis)
    spread = jnp.broadcast_to(x, (members,) + x.shape)
    return jnp.sum(lax.all_to_all(spread, axes, 0, 0, tiled=True), axis=0)


def solve_panel(rows, nearer, farther, inv_block, coupled):
    both = jnp.concatenate([nearer, farther], axis=1)
    total = rows.astype(jnp.float32) - jnp.dot(
        both, coupled, preferred_element_type=jnp.float32
    )
    return jnp.dot(
        total.astype(jnp.bfloat16), inv_block, preferred_element_type=jnp.float32
    ).astype(jnp.bfloat16)


def per_device(sources, forward, inv_diag, coupling, pattern):
    chips = lax.axis_size("chip")
    core = lax.axis_index("core")
    is_low = core == 0
    src_rows = sources.shape[0]
    half = src_rows // 2
    width = sources.shape[1]

    inv_block = inv_diag[0]
    weights = pattern[0].astype(coupling.dtype)
    weight_row = jnp.zeros((1, width), coupling.dtype).at[0, :2].set(weights)

    mine = lax.dynamic_slice_in_dim(sources, core * half, half, axis=0)
    mine_fwd = lax.dynamic_slice_in_dim(forward, core * half, half, axis=0)
    given = jnp.concatenate(
        [
            lax.dynamic_slice_in_dim(sources, (1 - core) * half, half, axis=0),
            lax.dynamic_slice_in_dim(forward, (1 - core) * half, half, axis=0),
            weight_row,
        ],
        axis=0,
    )
    other_coupling, other_inv, other_given = swapped(
        (coupling[0], inv_block, given), "core"
    )
    other_rows = other_given[:half]
    other_fwd = other_given[half : 2 * half]
    other_weights = other_given[2 * half, :2]

    def weighted(blocks, w):
        return jnp.concatenate([blocks[0] * w[0], blocks[1] * w[1]], axis=0)

    high_coupled = jnp.where(
        is_low, weighted(other_coupling, other_weights), weighted(coupling[0], weights)
    )
    low_coupled = jnp.where(
        is_low, weighted(coupling[0], weights), weighted(other_coupling, other_weights)
    )
    high_inv = jnp.where(is_low, other_inv, inv_block)
    high_rows = jnp.where(is_low, other_rows, mine)
    low_inv = jnp.where(is_low, inv_block, other_inv)
    low_rows = jnp.where(is_low, mine, other_rows)

    def both_panels(nearer, farther):
        high = solve_panel(high_rows, nearer, farther, high_inv, high_coupled)
        low = solve_panel(low_rows, high, nearer, low_inv, low_coupled)
        return low, high

    def sweep(step, carry):
        nearer, farther = carry
        low, high = both_panels(nearer, farther)
        packed = shifted(jnp.concatenate([low, high], axis=0), "chip", -1)
        return packed[:half], packed[half:]

    zeros_rows = jnp.zeros((half, width), jnp.bfloat16)
    nearer, farther = lax.fori_loop(0, chips - 1, sweep, (zeros_rows, zeros_rows))
    low, high = both_panels(nearer, farther)

    back = swapped(jnp.where(is_low, high, low), "core")
    adjoint = jnp.where(
        is_low,
        jnp.concatenate([low, back], axis=0),
        jnp.concatenate([back, high], axis=0),
    )

    high_fwd = jnp.where(is_low, other_fwd, mine_fwd)
    low_fwd = jnp.where(is_low, mine_fwd, other_fwd)
    partial_image = jnp.concatenate(
        [
            jnp.sum(low_fwd.astype(jnp.float32) * low.astype(jnp.float32), axis=0),
            jnp.sum(high_fwd.astype(jnp.float32) * high.astype(jnp.float32), axis=0),
        ]
    )
    grad = summed_over(partial_image, ("core", "src"))
    squares = summed_over(jnp.sum(grad * grad), ("chip",))
    count = float(chips * 2 * width)
    scale = jnp.sqrt(squares / count + 1e-06)
    direction = jnp.where(is_low, grad[:width], grad[width:]) / scale
    return (adjoint, direction)


def solution(mesh):
    chain = mesh.shape["chain"]
    src = mesh.shape["src"]
    devices = mesh.devices
    if mesh.axis_names != ("chain", "src"):
        devices = devices.T
    split = Mesh(devices.reshape(chain // 2, 2, src), ("chip", "core", "src"))
    return jax.shard_map(
        per_device,
        mesh=split,
        in_specs=(
            P("src", CHAIN),
            P("src", CHAIN),
            P(CHAIN, None, None),
            P(CHAIN, None, None, None),
            P(CHAIN, None),
        ),
        out_specs=(P("src", CHAIN), P(CHAIN)),
        check_vma=False,
    )
```

```python
import jax
import jax.numpy as jnp
from jax import lax
from jax.sharding import Mesh
from jax.sharding import PartitionSpec as P

CHAIN = ("chip", "core")


def shifted(x, axis, by):
    devices = lax.axis_size(axis)
    pairs = [(i, i + by) for i in range(devices) if 0 <= i + by < devices]
    return lax.ppermute(x, axis, pairs)


def swapped(x, axis):
    return lax.ppermute(x, axis, [(0, 1), (1, 0)])


def summed_over(x, axes):
    members = 1
    for axis in axes:
        members *= lax.axis_size(axis)
    spread = jnp.broadcast_to(x, (members,) + x.shape)
    return jnp.sum(lax.all_to_all(spread, axes, 0, 0, tiled=True), axis=0)


def solve_panel(rows, nearer, farther, inv_block, coupled):
    both = jnp.concatenate([nearer, farther], axis=1)
    total = rows.astype(jnp.float32) - jnp.dot(
        both, coupled, preferred_element_type=jnp.float32
    )
    return jnp.dot(
        total.astype(jnp.bfloat16), inv_block, preferred_element_type=jnp.float32
    ).astype(jnp.bfloat16)


def per_device(sources, forward, inv_diag, coupling, pattern):
    chips = lax.axis_size("chip")
    core = lax.axis_index("core")
    is_low = core == 0
    side = (core + lax.axis_index("chip")) % 2
    src_rows = sources.shape[0]
    half = src_rows // 2
    width = sources.shape[1]

    inv_block = inv_diag[0]
    weights = pattern[0].astype(coupling.dtype)
    weight_row = jnp.zeros((1, width), coupling.dtype).at[0, :2].set(weights)

    mine = lax.dynamic_slice_in_dim(sources, side * half, half, axis=0)
    mine_fwd = lax.dynamic_slice_in_dim(forward, side * half, half, axis=0)
    given = jnp.concatenate(
        [
            lax.dynamic_slice_in_dim(sources, (1 - side) * half, half, axis=0),
            lax.dynamic_slice_in_dim(forward, (1 - side) * half, half, axis=0),
            weight_row,
        ],
        axis=0,
    )
    other_coupling, other_inv, other_given = swapped(
        (coupling[0], inv_block, given), "core"
    )
    other_rows = other_given[:half]
    other_fwd = other_given[half : 2 * half]
    other_weights = other_given[2 * half, :2]

    def weighted(blocks, w):
        return jnp.concatenate([blocks[0] * w[0], blocks[1] * w[1]], axis=0)

    high_coupled = jnp.where(
        is_low, weighted(other_coupling, other_weights), weighted(coupling[0], weights)
    )
    low_coupled = jnp.where(
        is_low, weighted(coupling[0], weights), weighted(other_coupling, other_weights)
    )
    high_inv = jnp.where(is_low, other_inv, inv_block)
    high_rows = jnp.where(is_low, other_rows, mine)
    low_inv = jnp.where(is_low, inv_block, other_inv)
    low_rows = jnp.where(is_low, mine, other_rows)

    def both_panels(nearer, farther):
        high = solve_panel(high_rows, nearer, farther, high_inv, high_coupled)
        low = solve_panel(low_rows, high, nearer, low_inv, low_coupled)
        return low, high

    diagonal = [
        (2 * z + c, 2 * (z - 1) + 1 - c) for z in range(1, chips) for c in range(2)
    ]

    def sweep(step, carry):
        nearer, farther = carry
        low, high = both_panels(nearer, farther)
        packed = lax.ppermute(jnp.concatenate([low, high], axis=0), CHAIN, diagonal)
        return packed[:half], packed[half:]

    zeros_rows = jnp.zeros((half, width), jnp.bfloat16)
    nearer, farther = lax.fori_loop(0, chips - 1, sweep, (zeros_rows, zeros_rows))
    low, high = both_panels(nearer, farther)

    back = swapped(jnp.where(is_low, high, low), "core")
    own = jnp.where(is_low, low, high)
    adjoint = jnp.where(
        side == 0,
        jnp.concatenate([own, back], axis=0),
        jnp.concatenate([back, own], axis=0),
    )

    high_fwd = jnp.where(is_low, other_fwd, mine_fwd)
    low_fwd = jnp.where(is_low, mine_fwd, other_fwd)
    partial_image = jnp.concatenate(
        [
            jnp.sum(low_fwd.astype(jnp.float32) * low.astype(jnp.float32), axis=0),
            jnp.sum(high_fwd.astype(jnp.float32) * high.astype(jnp.float32), axis=0),
        ]
    )
    grad = summed_over(partial_image, ("core", "src"))
    squares = summed_over(jnp.sum(grad * grad), ("chip",))
    count = float(chips * 2 * width)
    scale = jnp.sqrt(squares / count + 1e-06)
    direction = jnp.where(is_low, grad[:width], grad[width:]) / scale
    return (adjoint, direction)


def solution(mesh):
    chain = mesh.shape["chain"]
    src = mesh.shape["src"]
    devices = mesh.devices
    if mesh.axis_names != ("chain", "src"):
        devices = devices.T
    split = Mesh(devices.reshape(chain // 2, 2, src), ("chip", "core", "src"))
    return jax.shard_map(
        per_device,
        mesh=split,
        in_specs=(
            P("src", CHAIN),
            P("src", CHAIN),
            P(CHAIN, None, None),
            P(CHAIN, None, None, None),
            P(CHAIN, None),
        ),
        out_specs=(P("src", CHAIN), P(CHAIN)),
        check_vma=False,
    )
```

```python
import jax
import jax.numpy as jnp
from jax import lax
from jax.sharding import Mesh
from jax.sharding import PartitionSpec as P

CHAIN = ("chip", "core")


def shifted(x, axis, by):
    devices = lax.axis_size(axis)
    pairs = [(i, i + by) for i in range(devices) if 0 <= i + by < devices]
    return lax.ppermute(x, axis, pairs)


def swapped(x, axis):
    return lax.ppermute(x, axis, [(0, 1), (1, 0)])


def summed_over(x, axes):
    members = 1
    for axis in axes:
        members *= lax.axis_size(axis)
    spread = jnp.broadcast_to(x, (members,) + x.shape)
    return jnp.sum(lax.all_to_all(spread, axes, 0, 0, tiled=True), axis=0)


def solve_panel(rows, nearer, farther, inv_block, coupled, weights):
    both = jnp.concatenate([nearer * weights[0], farther * weights[1]], axis=1)
    total = rows.astype(jnp.float32) - jnp.dot(
        both, coupled, preferred_element_type=jnp.float32
    )
    return jnp.dot(
        total.astype(jnp.bfloat16), inv_block, preferred_element_type=jnp.float32
    ).astype(jnp.bfloat16)


def per_device(sources, forward, inv_diag, coupling, pattern):
    chips = lax.axis_size("chip")
    core = lax.axis_index("core")
    is_low = core == 0
    side = (core + lax.axis_index("chip")) % 2
    src_rows = sources.shape[0]
    half = src_rows // 2
    width = sources.shape[1]

    inv_block = inv_diag[0]
    weights = pattern[0].astype(coupling.dtype)
    weight_row = jnp.zeros((1, width), coupling.dtype).at[0, :2].set(weights)

    mine = lax.dynamic_slice_in_dim(sources, side * half, half, axis=0)
    mine_fwd = lax.dynamic_slice_in_dim(forward, side * half, half, axis=0)
    given = jnp.concatenate(
        [
            lax.dynamic_slice_in_dim(sources, (1 - side) * half, half, axis=0),
            lax.dynamic_slice_in_dim(forward, (1 - side) * half, half, axis=0),
            weight_row,
        ],
        axis=0,
    )
    other_coupling, other_inv, other_given = swapped(
        (coupling[0], inv_block, given), "core"
    )
    other_rows = other_given[:half]
    other_fwd = other_given[half : 2 * half]
    other_weights = other_given[2 * half, :2]

    own_coupled = coupling[0].reshape(2 * width, width)
    other_coupled = other_coupling.reshape(2 * width, width)
    high_coupled = jnp.where(is_low, other_coupled, own_coupled)
    low_coupled = jnp.where(is_low, own_coupled, other_coupled)
    high_weights = jnp.where(is_low, other_weights, weights)
    low_weights = jnp.where(is_low, weights, other_weights)
    high_inv = jnp.where(is_low, other_inv, inv_block)
    high_rows = jnp.where(is_low, other_rows, mine)
    low_inv = jnp.where(is_low, inv_block, other_inv)
    low_rows = jnp.where(is_low, mine, other_rows)
    high_coupled, low_coupled, high_inv, low_inv = lax.optimization_barrier(
        (high_coupled, low_coupled, high_inv, low_inv)
    )

    def both_panels(nearer, farther):
        high = solve_panel(high_rows, nearer, farther, high_inv, high_coupled, high_weights)
        low = solve_panel(low_rows, high, nearer, low_inv, low_coupled, low_weights)
        return low, high

    diagonal = [
        (2 * z + c, 2 * (z - 1) + 1 - c) for z in range(1, chips) for c in range(2)
    ]

    def sweep(step, carry):
        nearer, farther = carry
        low, high = both_panels(nearer, farther)
        packed = lax.ppermute(jnp.concatenate([low, high], axis=0), CHAIN, diagonal)
        return packed[:half], packed[half:]

    zeros_rows = jnp.zeros((half, width), jnp.bfloat16)
    nearer, farther = lax.fori_loop(0, chips - 1, sweep, (zeros_rows, zeros_rows))
    low, high = both_panels(nearer, farther)

    back = swapped(jnp.where(is_low, high, low), "core")
    own = jnp.where(is_low, low, high)
    adjoint = jnp.where(
        side == 0,
        jnp.concatenate([own, back], axis=0),
        jnp.concatenate([back, own], axis=0),
    )

    high_fwd = jnp.where(is_low, other_fwd, mine_fwd)
    low_fwd = jnp.where(is_low, mine_fwd, other_fwd)
    partial_image = jnp.concatenate(
        [
            jnp.sum(low_fwd.astype(jnp.float32) * low.astype(jnp.float32), axis=0),
            jnp.sum(high_fwd.astype(jnp.float32) * high.astype(jnp.float32), axis=0),
        ]
    )
    grad = summed_over(partial_image, ("core", "src"))
    squares = summed_over(jnp.sum(grad * grad), ("chip",))
    count = float(chips * 2 * width)
    scale = jnp.sqrt(squares / count + 1e-06)
    direction = jnp.where(is_low, grad[:width], grad[width:]) / scale
    return (adjoint, direction)


def solution(mesh):
    chain = mesh.shape["chain"]
    src = mesh.shape["src"]
    devices = mesh.devices
    if mesh.axis_names != ("chain", "src"):
        devices = devices.T
    split = Mesh(devices.reshape(chain // 2, 2, src), ("chip", "core", "src"))
    return jax.shard_map(
        per_device,
        mesh=split,
        in_specs=(
            P("src", CHAIN),
            P("src", CHAIN),
            P(CHAIN, None, None),
            P(CHAIN, None, None, None),
            P(CHAIN, None),
        ),
        out_specs=(P("src", CHAIN), P(CHAIN)),
        check_vma=False,
    )
```

```python
import jax
import jax.numpy as jnp
from jax import lax
from jax.sharding import Mesh
from jax.sharding import PartitionSpec as P

CHAIN = ("chip", "core")


def shifted(x, axis, by):
    devices = lax.axis_size(axis)
    pairs = [(i, i + by) for i in range(devices) if 0 <= i + by < devices]
    return lax.ppermute(x, axis, pairs)


def swapped(x, axis):
    return lax.ppermute(x, axis, [(0, 1), (1, 0)])


def summed_over(x, axes):
    members = 1
    for axis in axes:
        members *= lax.axis_size(axis)
    spread = jnp.broadcast_to(x, (members,) + x.shape)
    return jnp.sum(lax.all_to_all(spread, axes, 0, 0, tiled=True), axis=0)


def solve_panel(rows, nearer, farther, inv_block, coupled):
    both = jnp.concatenate([nearer, farther], axis=1)
    total = rows.astype(jnp.float32) - jnp.dot(
        both, coupled, preferred_element_type=jnp.float32
    )
    return jnp.dot(
        total.astype(jnp.bfloat16), inv_block, preferred_element_type=jnp.float32
    ).astype(jnp.bfloat16)


def per_device(sources, forward, inv_diag, coupling, pattern):
    chips = lax.axis_size("chip")
    core = lax.axis_index("core")
    is_low = core == 0
    side = (core + lax.axis_index("chip")) % 2
    src_rows = sources.shape[0]
    half = src_rows // 2
    width = sources.shape[1]

    inv_block = inv_diag[0]
    weights = pattern[0].astype(coupling.dtype)
    weight_row = jnp.zeros((1, width), coupling.dtype).at[0, :2].set(weights)

    mine = lax.dynamic_slice_in_dim(sources, side * half, half, axis=0)
    mine_fwd = lax.dynamic_slice_in_dim(forward, side * half, half, axis=0)
    given = jnp.concatenate(
        [
            lax.dynamic_slice_in_dim(sources, (1 - side) * half, half, axis=0),
            lax.dynamic_slice_in_dim(forward, (1 - side) * half, half, axis=0),
            weight_row,
        ],
        axis=0,
    )
    other_coupling, other_inv, other_given = swapped(
        (coupling[0], inv_block, given), "core"
    )
    other_rows = other_given[:half]
    other_fwd = other_given[half : 2 * half]
    other_weights = other_given[2 * half, :2]

    def weighted(blocks, w):
        return jnp.concatenate([blocks[0] * w[0], blocks[1] * w[1]], axis=0)

    high_coupled = jnp.where(
        is_low, weighted(other_coupling, other_weights), weighted(coupling[0], weights)
    )
    low_coupled = jnp.where(
        is_low, weighted(coupling[0], weights), weighted(other_coupling, other_weights)
    )
    high_inv = jnp.where(is_low, other_inv, inv_block)
    high_rows = jnp.where(is_low, other_rows, mine)
    low_inv = jnp.where(is_low, inv_block, other_inv)
    low_rows = jnp.where(is_low, mine, other_rows)

    def both_panels(nearer, farther):
        high = solve_panel(high_rows, nearer, farther, high_inv, high_coupled)
        low = solve_panel(low_rows, high, nearer, low_inv, low_coupled)
        return low, high

    chip = lax.axis_index("chip")
    nearer = jnp.zeros((half, width), jnp.bfloat16)
    farther = nearer
    for step in range(chips - 1):
        low, high = both_panels(nearer, farther)
        sender = chips - 1 - step
        pairs = [(2 * sender + c, 2 * (sender - 1) + 1 - c) for c in range(2)]
        packed = lax.ppermute(jnp.concatenate([low, high], axis=0), CHAIN, pairs)
        taken = chip == sender - 1
        nearer = jnp.where(taken, packed[:half], nearer)
        farther = jnp.where(taken, packed[half:], farther)
    low, high = both_panels(nearer, farther)

    back = swapped(jnp.where(is_low, high, low), "core")
    own = jnp.where(is_low, low, high)
    adjoint = jnp.where(
        side == 0,
        jnp.concatenate([own, back], axis=0),
        jnp.concatenate([back, own], axis=0),
    )

    high_fwd = jnp.where(is_low, other_fwd, mine_fwd)
    low_fwd = jnp.where(is_low, mine_fwd, other_fwd)
    partial_image = jnp.concatenate(
        [
            jnp.sum(low_fwd.astype(jnp.float32) * low.astype(jnp.float32), axis=0),
            jnp.sum(high_fwd.astype(jnp.float32) * high.astype(jnp.float32), axis=0),
        ]
    )
    grad = summed_over(partial_image, ("core", "src"))
    squares = summed_over(jnp.sum(grad * grad), ("chip",))
    count = float(chips * 2 * width)
    scale = jnp.sqrt(squares / count + 1e-06)
    direction = jnp.where(is_low, grad[:width], grad[width:]) / scale
    return (adjoint, direction)


def solution(mesh):
    chain = mesh.shape["chain"]
    src = mesh.shape["src"]
    devices = mesh.devices
    if mesh.axis_names != ("chain", "src"):
        devices = devices.T
    split = Mesh(devices.reshape(chain // 2, 2, src), ("chip", "core", "src"))
    return jax.shard_map(
        per_device,
        mesh=split,
        in_specs=(
            P("src", CHAIN),
            P("src", CHAIN),
            P(CHAIN, None, None),
            P(CHAIN, None, None, None),
            P(CHAIN, None),
        ),
        out_specs=(P("src", CHAIN), P(CHAIN)),
        check_vma=False,
    )
```

```python
import jax
import jax.numpy as jnp
from jax import lax
from jax.sharding import Mesh
from jax.sharding import PartitionSpec as P

CHAIN = ("chip", "core")


def shifted(x, axis, by):
    devices = lax.axis_size(axis)
    pairs = [(i, i + by) for i in range(devices) if 0 <= i + by < devices]
    return lax.ppermute(x, axis, pairs)


def swapped(x, axis):
    return lax.ppermute(x, axis, [(0, 1), (1, 0)])


def summed_over(x, axes):
    members = 1
    for axis in axes:
        members *= lax.axis_size(axis)
    spread = jnp.broadcast_to(x, (members,) + x.shape)
    return jnp.sum(lax.all_to_all(spread, axes, 0, 0, tiled=True), axis=0)


def solve_panel(rows, nearer, farther, inv_block, coupled):
    both = jnp.concatenate([nearer, farther], axis=1)
    total = rows.astype(jnp.float32) - jnp.dot(
        both, coupled, preferred_element_type=jnp.float32
    )
    return jnp.dot(
        total.astype(jnp.bfloat16), inv_block, preferred_element_type=jnp.float32
    ).astype(jnp.bfloat16)


def per_device(sources, forward, inv_diag, coupling, pattern):
    chips = lax.axis_size("chip")
    core = lax.axis_index("core")
    is_low = core == 0
    side = (core + lax.axis_index("chip")) % 2
    src_rows = sources.shape[0]
    half = src_rows // 2
    width = sources.shape[1]

    inv_block = inv_diag[0]
    weights = pattern[0].astype(coupling.dtype)
    weight_row = jnp.zeros((1, width), coupling.dtype).at[0, :2].set(weights)

    mine = lax.dynamic_slice_in_dim(sources, side * half, half, axis=0)
    mine_fwd = lax.dynamic_slice_in_dim(forward, side * half, half, axis=0)
    given = jnp.concatenate(
        [
            lax.dynamic_slice_in_dim(sources, (1 - side) * half, half, axis=0),
            lax.dynamic_slice_in_dim(forward, (1 - side) * half, half, axis=0),
            weight_row,
        ],
        axis=0,
    )
    other_coupling, other_inv, other_given = swapped(
        (coupling[0], inv_block, given), "core"
    )
    other_rows = other_given[:half]
    other_fwd = other_given[half : 2 * half]
    other_weights = other_given[2 * half, :2]

    def weighted(blocks, w):
        return jnp.concatenate([blocks[0] * w[0], blocks[1] * w[1]], axis=0)

    high_coupled = jnp.where(
        is_low, weighted(other_coupling, other_weights), weighted(coupling[0], weights)
    )
    low_coupled = jnp.where(
        is_low, weighted(coupling[0], weights), weighted(other_coupling, other_weights)
    )
    high_inv = jnp.where(is_low, other_inv, inv_block)
    high_rows = jnp.where(is_low, other_rows, mine)
    low_inv = jnp.where(is_low, inv_block, other_inv)
    low_rows = jnp.where(is_low, mine, other_rows)

    def both_panels(nearer, farther):
        high = solve_panel(high_rows, nearer, farther, high_inv, high_coupled)
        low = solve_panel(low_rows, high, nearer, low_inv, low_coupled)
        return low, high

    chip = lax.axis_index("chip")
    nearer = jnp.zeros((half, width), jnp.bfloat16)
    farther = nearer
    kept_low = nearer
    kept_high = nearer
    for step in range(chips):
        low, high = both_panels(nearer, farther)
        sender = chips - 1 - step
        if sender > 0:
            pairs = [(2 * sender + c, 2 * (sender - 1) + 1 - c) for c in range(2)]
            packed = lax.ppermute(
                jnp.concatenate([low, high], axis=0), CHAIN, pairs
            )
            nearer, farther = packed[:half], packed[half:]
        final = chip == sender
        kept_low = jnp.where(final, low, kept_low)
        kept_high = jnp.where(final, high, kept_high)
    low, high = kept_low, kept_high

    back = swapped(jnp.where(is_low, high, low), "core")
    own = jnp.where(is_low, low, high)
    adjoint = jnp.where(
        side == 0,
        jnp.concatenate([own, back], axis=0),
        jnp.concatenate([back, own], axis=0),
    )

    high_fwd = jnp.where(is_low, other_fwd, mine_fwd)
    low_fwd = jnp.where(is_low, mine_fwd, other_fwd)
    partial_image = jnp.concatenate(
        [
            jnp.sum(low_fwd.astype(jnp.float32) * low.astype(jnp.float32), axis=0),
            jnp.sum(high_fwd.astype(jnp.float32) * high.astype(jnp.float32), axis=0),
        ]
    )
    grad = summed_over(partial_image, ("core", "src"))
    squares = summed_over(jnp.sum(grad * grad), ("chip",))
    count = float(chips * 2 * width)
    scale = jnp.sqrt(squares / count + 1e-06)
    direction = jnp.where(is_low, grad[:width], grad[width:]) / scale
    return (adjoint, direction)


def solution(mesh):
    chain = mesh.shape["chain"]
    src = mesh.shape["src"]
    devices = mesh.devices
    if mesh.axis_names != ("chain", "src"):
        devices = devices.T
    split = Mesh(devices.reshape(chain // 2, 2, src), ("chip", "core", "src"))
    return jax.shard_map(
        per_device,
        mesh=split,
        in_specs=(
            P("src", CHAIN),
            P("src", CHAIN),
            P(CHAIN, None, None),
            P(CHAIN, None, None, None),
            P(CHAIN, None),
        ),
        out_specs=(P("src", CHAIN), P(CHAIN)),
        check_vma=False,
    )
```

```python
import jax
import jax.numpy as jnp
from jax import lax
from jax.sharding import Mesh
from jax.sharding import PartitionSpec as P

CHAIN = ("chip", "core")


def shifted(x, axis, by):
    devices = lax.axis_size(axis)
    pairs = [(i, i + by) for i in range(devices) if 0 <= i + by < devices]
    return lax.ppermute(x, axis, pairs)


def swapped(x, axis):
    return lax.ppermute(x, axis, [(0, 1), (1, 0)])


def summed_over(x, axes):
    members = 1
    for axis in axes:
        members *= lax.axis_size(axis)
    spread = jnp.broadcast_to(x, (members,) + x.shape)
    return jnp.sum(lax.all_to_all(spread, axes, 0, 0, tiled=True), axis=0)


def solve_panel(rows, both, inv_block, coupled):
    total = rows.astype(jnp.float32) - jnp.dot(
        both, coupled, preferred_element_type=jnp.float32
    )
    return jnp.dot(
        total.astype(jnp.bfloat16), inv_block, preferred_element_type=jnp.float32
    ).astype(jnp.bfloat16)


def per_device(sources, forward, inv_diag, coupling, pattern):
    chips = lax.axis_size("chip")
    core = lax.axis_index("core")
    is_low = core == 0
    side = (core + lax.axis_index("chip")) % 2
    src_rows = sources.shape[0]
    half = src_rows // 2
    width = sources.shape[1]

    inv_block = inv_diag[0]
    weights = pattern[0].astype(coupling.dtype)
    weight_row = jnp.zeros((1, width), coupling.dtype).at[0, :2].set(weights)

    mine = lax.dynamic_slice_in_dim(sources, side * half, half, axis=0)
    mine_fwd = lax.dynamic_slice_in_dim(forward, side * half, half, axis=0)
    given = jnp.concatenate(
        [
            lax.dynamic_slice_in_dim(sources, (1 - side) * half, half, axis=0),
            lax.dynamic_slice_in_dim(forward, (1 - side) * half, half, axis=0),
            weight_row,
        ],
        axis=0,
    )
    other_coupling, other_inv, other_given = swapped(
        (coupling[0], inv_block, given), "core"
    )
    other_rows = other_given[:half]
    other_fwd = other_given[half : 2 * half]
    other_weights = other_given[2 * half, :2]

    def weighted(blocks, w):
        return jnp.concatenate([blocks[0] * w[0], blocks[1] * w[1]], axis=0)

    high_coupled = jnp.where(
        is_low, weighted(other_coupling, other_weights), weighted(coupling[0], weights)
    )
    low_coupled = jnp.where(
        is_low, weighted(coupling[0], weights), weighted(other_coupling, other_weights)
    )
    high_inv = jnp.where(is_low, other_inv, inv_block)
    high_rows = jnp.where(is_low, other_rows, mine)
    low_inv = jnp.where(is_low, inv_block, other_inv)
    low_rows = jnp.where(is_low, mine, other_rows)

    def both_panels(message):
        high = solve_panel(high_rows, message, high_inv, high_coupled)
        nearer = message[:, :width]
        low = solve_panel(
            low_rows, jnp.concatenate([high, nearer], axis=1), low_inv, low_coupled
        )
        return low, high

    chip = lax.axis_index("chip")
    message = jnp.zeros((half, 2 * width), jnp.bfloat16)
    kept = message
    for step in range(chips - 1):
        low, high = both_panels(message)
        if step > 0:
            low, high, message = lax.optimization_barrier((low, high, message))
            kept = jnp.where(chip == chips - 1 - step, message, kept)
        sender = chips - 1 - step
        pairs = [(2 * sender + c, 2 * (sender - 1) + 1 - c) for c in range(2)]
        message = lax.ppermute(jnp.concatenate([low, high], axis=1), CHAIN, pairs)
    kept = jnp.where(chip == 0, message, kept)
    low, high = both_panels(kept)

    back = swapped(jnp.where(is_low, high, low), "core")
    own = jnp.where(is_low, low, high)
    adjoint = jnp.where(
        side == 0,
        jnp.concatenate([own, back], axis=0),
        jnp.concatenate([back, own], axis=0),
    )

    high_fwd = jnp.where(is_low, other_fwd, mine_fwd)
    low_fwd = jnp.where(is_low, mine_fwd, other_fwd)
    partial_image = jnp.concatenate(
        [
            jnp.sum(low_fwd.astype(jnp.float32) * low.astype(jnp.float32), axis=0),
            jnp.sum(high_fwd.astype(jnp.float32) * high.astype(jnp.float32), axis=0),
        ]
    )
    grad = summed_over(partial_image, ("core", "src"))
    squares = summed_over(jnp.sum(grad * grad), ("chip",))
    count = float(chips * 2 * width)
    scale = jnp.sqrt(squares / count + 1e-06)
    direction = jnp.where(is_low, grad[:width], grad[width:]) / scale
    return (adjoint, direction)


def solution(mesh):
    chain = mesh.shape["chain"]
    src = mesh.shape["src"]
    devices = mesh.devices
    if mesh.axis_names != ("chain", "src"):
        devices = devices.T
    split = Mesh(devices.reshape(chain // 2, 2, src), ("chip", "core", "src"))
    return jax.shard_map(
        per_device,
        mesh=split,
        in_specs=(
            P("src", CHAIN),
            P("src", CHAIN),
            P(CHAIN, None, None),
            P(CHAIN, None, None, None),
            P(CHAIN, None),
        ),
        out_specs=(P("src", CHAIN), P(CHAIN)),
        check_vma=False,
    )
```

```python
import jax
import jax.numpy as jnp
from jax import lax
from jax.sharding import Mesh
from jax.sharding import PartitionSpec as P

CHAIN = ("chip", "core")


def shifted(x, axis, by):
    devices = lax.axis_size(axis)
    pairs = [(i, i + by) for i in range(devices) if 0 <= i + by < devices]
    return lax.ppermute(x, axis, pairs)


def swapped(x, axis):
    return lax.ppermute(x, axis, [(0, 1), (1, 0)])


def summed_over(x, axes):
    members = 1
    for axis in axes:
        members *= lax.axis_size(axis)
    spread = jnp.broadcast_to(x, (members,) + x.shape)
    return jnp.sum(lax.all_to_all(spread, axes, 0, 0, tiled=True), axis=0)


def solve_panel(rows, nearer, farther, inv_block, coupled):
    both = jnp.concatenate([nearer, farther], axis=1)
    total = rows.astype(jnp.float32) - jnp.dot(
        both, coupled, preferred_element_type=jnp.float32
    )
    return jnp.dot(
        total.astype(jnp.bfloat16), inv_block, preferred_element_type=jnp.float32
    ).astype(jnp.bfloat16)


def per_device(sources, forward, inv_diag, coupling, pattern):
    chips = lax.axis_size("chip")
    core = lax.axis_index("core")
    is_low = core == 0
    side = (core + lax.axis_index("chip")) % 2
    src_rows = sources.shape[0]
    half = src_rows // 2
    width = sources.shape[1]

    inv_block = inv_diag[0]
    weights = pattern[0].astype(coupling.dtype)
    weight_row = jnp.zeros((1, width), coupling.dtype).at[0, :2].set(weights)

    mine = lax.dynamic_slice_in_dim(sources, side * half, half, axis=0)
    mine_fwd = lax.dynamic_slice_in_dim(forward, side * half, half, axis=0)
    given = jnp.concatenate(
        [
            lax.dynamic_slice_in_dim(sources, (1 - side) * half, half, axis=0),
            lax.dynamic_slice_in_dim(forward, (1 - side) * half, half, axis=0),
            weight_row,
        ],
        axis=0,
    )
    other_coupling, other_inv, other_given = swapped(
        (coupling[0], inv_block, given), "core"
    )
    other_rows = other_given[:half]
    other_fwd = other_given[half : 2 * half]
    other_weights = other_given[2 * half, :2]

    def weighted(blocks, w):
        return jnp.concatenate([blocks[0] * w[0], blocks[1] * w[1]], axis=0)

    high_coupled = jnp.where(
        is_low, weighted(other_coupling, other_weights), weighted(coupling[0], weights)
    )
    low_coupled = jnp.where(
        is_low, weighted(coupling[0], weights), weighted(other_coupling, other_weights)
    )
    high_inv = jnp.where(is_low, other_inv, inv_block)
    high_rows = jnp.where(is_low, other_rows, mine)
    low_inv = jnp.where(is_low, inv_block, other_inv)
    low_rows = jnp.where(is_low, mine, other_rows)

    def both_panels(nearer, farther):
        high = solve_panel(high_rows, nearer, farther, high_inv, high_coupled)
        low = solve_panel(low_rows, high, nearer, low_inv, low_coupled)
        return low, high

    def composed(coupled, inv):
        product = jnp.dot(coupled, inv, preferred_element_type=jnp.float32)
        return product.astype(jnp.bfloat16)

    def composed_panels(nearer, farther, parts):
        high_shift, high_map, low_shift, low_map = parts
        both = jnp.concatenate([nearer, farther], axis=1)
        high = (high_shift - jnp.dot(both, high_map, preferred_element_type=jnp.float32)).astype(jnp.bfloat16)
        both = jnp.concatenate([high, nearer], axis=1)
        low = (low_shift - jnp.dot(both, low_map, preferred_element_type=jnp.float32)).astype(jnp.bfloat16)
        return low, high

    chip = lax.axis_index("chip")
    nearer = jnp.zeros((half, width), jnp.bfloat16)
    farther = nearer
    parts = None
    for step in range(chips - 1):
        if parts is None:
            low, high = both_panels(nearer, farther)
        else:
            low, high = composed_panels(nearer, farther, parts)
        sender = chips - 1 - step
        pairs = [(2 * sender + c, 2 * (sender - 1) + 1 - c) for c in range(2)]
        packed = lax.ppermute(jnp.concatenate([low, high], axis=0), CHAIN, pairs)
        if parts is None:
            parts = (
                jnp.dot(high_rows, high_inv, preferred_element_type=jnp.float32),
                composed(high_coupled, high_inv),
                jnp.dot(low_rows, low_inv, preferred_element_type=jnp.float32),
                composed(low_coupled, low_inv),
            )
        taken = chip == sender - 1
        nearer = jnp.where(taken, packed[:half], nearer)
        farther = jnp.where(taken, packed[half:], farther)
    low, high = composed_panels(nearer, farther, parts)

    back = swapped(jnp.where(is_low, high, low), "core")
    own = jnp.where(is_low, low, high)
    adjoint = jnp.where(
        side == 0,
        jnp.concatenate([own, back], axis=0),
        jnp.concatenate([back, own], axis=0),
    )

    high_fwd = jnp.where(is_low, other_fwd, mine_fwd)
    low_fwd = jnp.where(is_low, mine_fwd, other_fwd)
    partial_image = jnp.concatenate(
        [
            jnp.sum(low_fwd.astype(jnp.float32) * low.astype(jnp.float32), axis=0),
            jnp.sum(high_fwd.astype(jnp.float32) * high.astype(jnp.float32), axis=0),
        ]
    )
    grad = summed_over(partial_image, ("core", "src"))
    squares = summed_over(jnp.sum(grad * grad), ("chip",))
    count = float(chips * 2 * width)
    scale = jnp.sqrt(squares / count + 1e-06)
    direction = jnp.where(is_low, grad[:width], grad[width:]) / scale
    return (adjoint, direction)


def solution(mesh):
    chain = mesh.shape["chain"]
    src = mesh.shape["src"]
    devices = mesh.devices
    if mesh.axis_names != ("chain", "src"):
        devices = devices.T
    split = Mesh(devices.reshape(chain // 2, 2, src), ("chip", "core", "src"))
    return jax.shard_map(
        per_device,
        mesh=split,
        in_specs=(
            P("src", CHAIN),
            P("src", CHAIN),
            P(CHAIN, None, None),
            P(CHAIN, None, None, None),
            P(CHAIN, None),
        ),
        out_specs=(P("src", CHAIN), P(CHAIN)),
        check_vma=False,
    )
```

```python
import jax
import jax.numpy as jnp
from jax import lax
from jax.sharding import Mesh
from jax.sharding import PartitionSpec as P

CHAIN = ("chip", "core")


def shifted(x, axis, by):
    devices = lax.axis_size(axis)
    pairs = [(i, i + by) for i in range(devices) if 0 <= i + by < devices]
    return lax.ppermute(x, axis, pairs)


def swapped(x, axis):
    return lax.ppermute(x, axis, [(0, 1), (1, 0)])


def summed_over(x, axes):
    members = 1
    for axis in axes:
        members *= lax.axis_size(axis)
    spread = jnp.broadcast_to(x, (members,) + x.shape)
    return jnp.sum(lax.all_to_all(spread, axes, 0, 0, tiled=True), axis=0)


def solve_panel(rows, nearer, farther, inv_block, coupled):
    both = jnp.concatenate([nearer, farther], axis=1)
    total = rows.astype(jnp.float32) - jnp.dot(
        both, coupled, preferred_element_type=jnp.float32
    )
    return jnp.dot(
        total.astype(jnp.bfloat16), inv_block, preferred_element_type=jnp.float32
    ).astype(jnp.bfloat16)


def per_device(sources, forward, inv_diag, coupling, pattern):
    chips = lax.axis_size("chip")
    core = lax.axis_index("core")
    is_low = core == 0
    side = (core + lax.axis_index("chip")) % 2
    src_rows = sources.shape[0]
    half = src_rows // 2
    width = sources.shape[1]

    inv_block = inv_diag[0]
    weights = pattern[0].astype(coupling.dtype)
    weight_row = jnp.zeros((1, width), coupling.dtype).at[0, :2].set(weights)

    mine = lax.dynamic_slice_in_dim(sources, side * half, half, axis=0)
    mine_fwd = lax.dynamic_slice_in_dim(forward, side * half, half, axis=0)
    given = jnp.concatenate(
        [
            lax.dynamic_slice_in_dim(sources, (1 - side) * half, half, axis=0),
            lax.dynamic_slice_in_dim(forward, (1 - side) * half, half, axis=0),
            weight_row,
        ],
        axis=0,
    )
    other_coupling, other_inv, other_given = swapped(
        (coupling[0], inv_block, given), "core"
    )
    other_rows = other_given[:half]
    other_fwd = other_given[half : 2 * half]
    other_weights = other_given[2 * half, :2]

    def weighted(blocks, w):
        return jnp.concatenate([blocks[0] * w[0], blocks[1] * w[1]], axis=0)

    high_coupled = jnp.where(
        is_low, weighted(other_coupling, other_weights), weighted(coupling[0], weights)
    )
    low_coupled = jnp.where(
        is_low, weighted(coupling[0], weights), weighted(other_coupling, other_weights)
    )
    high_inv = jnp.where(is_low, other_inv, inv_block)
    high_rows = jnp.where(is_low, other_rows, mine)
    low_inv = jnp.where(is_low, inv_block, other_inv)
    low_rows = jnp.where(is_low, mine, other_rows)

    def both_panels(nearer, farther):
        high = solve_panel(high_rows, nearer, farther, high_inv, high_coupled)
        low = solve_panel(low_rows, high, nearer, low_inv, low_coupled)
        return low, high

    def composed(coupled, inv):
        product = jnp.dot(coupled, inv, preferred_element_type=jnp.float32)
        return product.astype(jnp.bfloat16)

    def composed_panels(nearer, farther, parts):
        high_shift, high_map, low_shift, low_map = parts
        both = jnp.concatenate([nearer, farther], axis=1)
        high = (high_shift - jnp.dot(both, high_map, preferred_element_type=jnp.float32)).astype(jnp.bfloat16)
        both = jnp.concatenate([high, nearer], axis=1)
        low = (low_shift - jnp.dot(both, low_map, preferred_element_type=jnp.float32)).astype(jnp.bfloat16)
        return low, high

    chip = lax.axis_index("chip")
    nearer = jnp.zeros((half, width), jnp.bfloat16)
    farther = nearer
    parts = None
    for step in range(chips - 1):
        if parts is None:
            high = jnp.dot(
                high_rows, high_inv, preferred_element_type=jnp.float32
            ).astype(jnp.bfloat16)
            total = low_rows.astype(jnp.float32) - jnp.dot(
                high, low_coupled[:width], preferred_element_type=jnp.float32
            )
            low = jnp.dot(
                total.astype(jnp.bfloat16), low_inv, preferred_element_type=jnp.float32
            ).astype(jnp.bfloat16)
        else:
            low, high = composed_panels(nearer, farther, parts)
        sender = chips - 1 - step
        pairs = [(2 * sender + c, 2 * (sender - 1) + 1 - c) for c in range(2)]
        packed = lax.ppermute(jnp.concatenate([low, high], axis=0), CHAIN, pairs)
        if parts is None:
            parts = (
                jnp.dot(high_rows, high_inv, preferred_element_type=jnp.float32),
                composed(high_coupled, high_inv),
                jnp.dot(low_rows, low_inv, preferred_element_type=jnp.float32),
                composed(low_coupled, low_inv),
            )
        taken = chip == sender - 1
        nearer = jnp.where(taken, packed[:half], nearer)
        farther = jnp.where(taken, packed[half:], farther)
    low, high = composed_panels(nearer, farther, parts)

    back = swapped(jnp.where(is_low, high, low), "core")
    own = jnp.where(is_low, low, high)
    adjoint = jnp.where(
        side == 0,
        jnp.concatenate([own, back], axis=0),
        jnp.concatenate([back, own], axis=0),
    )

    high_fwd = jnp.where(is_low, other_fwd, mine_fwd)
    low_fwd = jnp.where(is_low, mine_fwd, other_fwd)
    partial_image = jnp.concatenate(
        [
            jnp.sum(low_fwd.astype(jnp.float32) * low.astype(jnp.float32), axis=0),
            jnp.sum(high_fwd.astype(jnp.float32) * high.astype(jnp.float32), axis=0),
        ]
    )
    grad = summed_over(partial_image, ("core", "src"))
    squares = summed_over(jnp.sum(grad * grad), ("chip",))
    count = float(chips * 2 * width)
    scale = jnp.sqrt(squares / count + 1e-06)
    direction = jnp.where(is_low, grad[:width], grad[width:]) / scale
    return (adjoint, direction)


def solution(mesh):
    chain = mesh.shape["chain"]
    src = mesh.shape["src"]
    devices = mesh.devices
    if mesh.axis_names != ("chain", "src"):
        devices = devices.T
    split = Mesh(devices.reshape(chain // 2, 2, src), ("chip", "core", "src"))
    return jax.shard_map(
        per_device,
        mesh=split,
        in_specs=(
            P("src", CHAIN),
            P("src", CHAIN),
            P(CHAIN, None, None),
            P(CHAIN, None, None, None),
            P(CHAIN, None),
        ),
        out_specs=(P("src", CHAIN), P(CHAIN)),
        check_vma=False,
    )
```

```python
import jax
import jax.numpy as jnp
from jax import lax
from jax.sharding import Mesh
from jax.sharding import PartitionSpec as P

CHAIN = ("chip", "core")


def shifted(x, axis, by):
    devices = lax.axis_size(axis)
    pairs = [(i, i + by) for i in range(devices) if 0 <= i + by < devices]
    return lax.ppermute(x, axis, pairs)


def swapped(x, axis):
    return lax.ppermute(x, axis, [(0, 1), (1, 0)])


def summed_over(x, axes):
    members = 1
    for axis in axes:
        members *= lax.axis_size(axis)
    spread = jnp.broadcast_to(x, (members,) + x.shape)
    return jnp.sum(lax.all_to_all(spread, axes, 0, 0, tiled=True), axis=0)


def solve_panel(rows, nearer, farther, inv_block, coupled):
    both = jnp.concatenate([nearer, farther], axis=1)
    total = rows.astype(jnp.float32) - jnp.dot(
        both, coupled, preferred_element_type=jnp.float32
    )
    return jnp.dot(
        total.astype(jnp.bfloat16), inv_block, preferred_element_type=jnp.float32
    ).astype(jnp.bfloat16)


def per_device(sources, forward, inv_diag, coupling, pattern):
    chips = lax.axis_size("chip")
    core = lax.axis_index("core")
    is_low = core == 0
    side = (core + lax.axis_index("chip")) % 2
    src_rows = sources.shape[0]
    half = src_rows // 2
    width = sources.shape[1]

    inv_block = inv_diag[0]
    weights = pattern[0].astype(coupling.dtype)
    weight_row = jnp.zeros((1, width), coupling.dtype).at[0, :2].set(weights)

    mine = lax.dynamic_slice_in_dim(sources, side * half, half, axis=0)
    mine_fwd = lax.dynamic_slice_in_dim(forward, side * half, half, axis=0)
    given = jnp.concatenate(
        [
            lax.dynamic_slice_in_dim(sources, (1 - side) * half, half, axis=0),
            lax.dynamic_slice_in_dim(forward, (1 - side) * half, half, axis=0),
            weight_row,
        ],
        axis=0,
    )
    other_coupling, other_inv, other_given = swapped(
        (coupling[0], inv_block, given), "core"
    )
    other_rows = other_given[:half]
    other_fwd = other_given[half : 2 * half]
    other_weights = other_given[2 * half, :2]

    def weighted(blocks, w):
        return jnp.concatenate([blocks[0] * w[0], blocks[1] * w[1]], axis=0)

    first_low = jnp.where(
        is_low, coupling[0, 0] * weights[0], other_coupling[0] * other_weights[0]
    )
    high_inv = jnp.where(is_low, other_inv, inv_block)
    high_rows = jnp.where(is_low, other_rows, mine)
    low_inv = jnp.where(is_low, inv_block, other_inv)
    low_rows = jnp.where(is_low, mine, other_rows)

    def both_panels(nearer, farther):
        high = solve_panel(high_rows, nearer, farther, high_inv, high_coupled)
        low = solve_panel(low_rows, high, nearer, low_inv, low_coupled)
        return low, high

    def composed(coupled, inv):
        product = jnp.dot(coupled, inv, preferred_element_type=jnp.float32)
        return product.astype(jnp.bfloat16)

    def composed_panels(nearer, farther, parts):
        high_shift, high_map, low_shift, low_map = parts
        both = jnp.concatenate([nearer, farther], axis=1)
        high = (high_shift - jnp.dot(both, high_map, preferred_element_type=jnp.float32)).astype(jnp.bfloat16)
        both = jnp.concatenate([high, nearer], axis=1)
        low = (low_shift - jnp.dot(both, low_map, preferred_element_type=jnp.float32)).astype(jnp.bfloat16)
        return low, high

    chip = lax.axis_index("chip")
    nearer = jnp.zeros((half, width), jnp.bfloat16)
    farther = nearer
    parts = None
    for step in range(chips - 1):
        if parts is None:
            high = jnp.dot(
                high_rows, high_inv, preferred_element_type=jnp.float32
            ).astype(jnp.bfloat16)
            total = low_rows.astype(jnp.float32) - jnp.dot(
                high, first_low, preferred_element_type=jnp.float32
            )
            low = jnp.dot(
                total.astype(jnp.bfloat16), low_inv, preferred_element_type=jnp.float32
            ).astype(jnp.bfloat16)
        else:
            low, high = composed_panels(nearer, farther, parts)
        sender = chips - 1 - step
        pairs = [(2 * sender + c, 2 * (sender - 1) + 1 - c) for c in range(2)]
        packed = lax.ppermute(jnp.concatenate([low, high], axis=0), CHAIN, pairs)
        if parts is None:
            own_blocks, other_blocks, _ = lax.optimization_barrier(
                (coupling[0], other_coupling, low)
            )
            high_coupled = jnp.where(
                is_low,
                weighted(other_blocks, other_weights),
                weighted(own_blocks, weights),
            )
            low_coupled = jnp.where(
                is_low,
                weighted(own_blocks, weights),
                weighted(other_blocks, other_weights),
            )
            parts = (
                jnp.dot(high_rows, high_inv, preferred_element_type=jnp.float32),
                composed(high_coupled, high_inv),
                jnp.dot(low_rows, low_inv, preferred_element_type=jnp.float32),
                composed(low_coupled, low_inv),
            )
        taken = chip == sender - 1
        nearer = jnp.where(taken, packed[:half], nearer)
        farther = jnp.where(taken, packed[half:], farther)
    low, high = composed_panels(nearer, farther, parts)

    back = swapped(jnp.where(is_low, high, low), "core")
    own = jnp.where(is_low, low, high)
    adjoint = jnp.where(
        side == 0,
        jnp.concatenate([own, back], axis=0),
        jnp.concatenate([back, own], axis=0),
    )

    high_fwd = jnp.where(is_low, other_fwd, mine_fwd)
    low_fwd = jnp.where(is_low, mine_fwd, other_fwd)
    partial_image = jnp.concatenate(
        [
            jnp.sum(low_fwd.astype(jnp.float32) * low.astype(jnp.float32), axis=0),
            jnp.sum(high_fwd.astype(jnp.float32) * high.astype(jnp.float32), axis=0),
        ]
    )
    grad = summed_over(partial_image, ("core", "src"))
    squares = summed_over(jnp.sum(grad * grad), ("chip",))
    count = float(chips * 2 * width)
    scale = jnp.sqrt(squares / count + 1e-06)
    direction = jnp.where(is_low, grad[:width], grad[width:]) / scale
    return (adjoint, direction)


def solution(mesh):
    chain = mesh.shape["chain"]
    src = mesh.shape["src"]
    devices = mesh.devices
    if mesh.axis_names != ("chain", "src"):
        devices = devices.T
    split = Mesh(devices.reshape(chain // 2, 2, src), ("chip", "core", "src"))
    return jax.shard_map(
        per_device,
        mesh=split,
        in_specs=(
            P("src", CHAIN),
            P("src", CHAIN),
            P(CHAIN, None, None),
            P(CHAIN, None, None, None),
            P(CHAIN, None),
        ),
        out_specs=(P("src", CHAIN), P(CHAIN)),
        check_vma=False,
    )
```

```python
import jax
import jax.numpy as jnp
from jax import lax
from jax.sharding import Mesh
from jax.sharding import PartitionSpec as P

CHAIN = ("chip", "core")


def shifted(x, axis, by):
    devices = lax.axis_size(axis)
    pairs = [(i, i + by) for i in range(devices) if 0 <= i + by < devices]
    return lax.ppermute(x, axis, pairs)


def swapped(x, axis):
    return lax.ppermute(x, axis, [(0, 1), (1, 0)])


def summed_over(x, axes):
    members = 1
    for axis in axes:
        members *= lax.axis_size(axis)
    spread = jnp.broadcast_to(x, (members,) + x.shape)
    return jnp.sum(lax.all_to_all(spread, axes, 0, 0, tiled=True), axis=0)


def solve_panel(rows, nearer, farther, inv_block, coupled):
    both = jnp.concatenate([nearer, farther], axis=1)
    total = rows.astype(jnp.float32) - jnp.dot(
        both, coupled, preferred_element_type=jnp.float32
    )
    return jnp.dot(
        total.astype(jnp.bfloat16), inv_block, preferred_element_type=jnp.float32
    ).astype(jnp.bfloat16)


def per_device(sources, forward, inv_diag, coupling, pattern):
    chips = lax.axis_size("chip")
    core = lax.axis_index("core")
    is_low = core == 0
    side = (core + lax.axis_index("chip")) % 2
    src_rows = sources.shape[0]
    half = src_rows // 2
    width = sources.shape[1]

    inv_block = inv_diag[0]
    weights = pattern[0].astype(coupling.dtype)
    weight_row = jnp.zeros((1, width), coupling.dtype).at[0, :2].set(weights)

    mine = lax.dynamic_slice_in_dim(sources, side * half, half, axis=0)
    mine_fwd = lax.dynamic_slice_in_dim(forward, side * half, half, axis=0)
    given = jnp.concatenate(
        [
            lax.dynamic_slice_in_dim(sources, (1 - side) * half, half, axis=0),
            lax.dynamic_slice_in_dim(forward, (1 - side) * half, half, axis=0),
            weight_row,
        ],
        axis=0,
    )
    other_coupling, other_inv, other_given = swapped(
        (coupling[0], inv_block, given), "core"
    )
    other_rows = other_given[:half]
    other_fwd = other_given[half : 2 * half]
    other_weights = other_given[2 * half, :2]

    def weighted(blocks, w):
        return jnp.concatenate([blocks[0] * w[0], blocks[1] * w[1]], axis=0)

    first_low = jnp.where(
        is_low, coupling[0, 0] * weights[0], other_coupling[0] * other_weights[0]
    )
    high_inv = jnp.where(is_low, other_inv, inv_block)
    high_rows = jnp.where(is_low, other_rows, mine)
    low_inv = jnp.where(is_low, inv_block, other_inv)
    low_rows = jnp.where(is_low, mine, other_rows)

    def both_panels(nearer, farther, high_coupled, low_coupled):
        high = solve_panel(high_rows, nearer, farther, high_inv, high_coupled)
        low = solve_panel(low_rows, high, nearer, low_inv, low_coupled)
        return low, high

    def composed(coupled, inv):
        product = jnp.dot(coupled, inv, preferred_element_type=jnp.float32)
        return product.astype(jnp.bfloat16)

    def composed_panels(nearer, farther, parts):
        high_shift, high_map, low_shift, low_map = parts
        both = jnp.concatenate([nearer, farther], axis=1)
        high = (high_shift - jnp.dot(both, high_map, preferred_element_type=jnp.float32)).astype(jnp.bfloat16)
        both = jnp.concatenate([high, nearer], axis=1)
        low = (low_shift - jnp.dot(both, low_map, preferred_element_type=jnp.float32)).astype(jnp.bfloat16)
        return low, high

    chip = lax.axis_index("chip")
    nearer = jnp.zeros((half, width), jnp.bfloat16)
    farther = nearer
    parts = None
    for step in range(chips - 1):
        if step == 0:
            high = jnp.dot(
                high_rows, high_inv, preferred_element_type=jnp.float32
            ).astype(jnp.bfloat16)
            total = low_rows.astype(jnp.float32) - jnp.dot(
                high, first_low, preferred_element_type=jnp.float32
            )
            low = jnp.dot(
                total.astype(jnp.bfloat16), low_inv, preferred_element_type=jnp.float32
            ).astype(jnp.bfloat16)
        elif step == 1:
            low, high = both_panels(nearer, farther, high_coupled, low_coupled)
        else:
            low, high = composed_panels(nearer, farther, parts)
        sender = chips - 1 - step
        pairs = [(2 * sender + c, 2 * (sender - 1) + 1 - c) for c in range(2)]
        packed = lax.ppermute(jnp.concatenate([low, high], axis=0), CHAIN, pairs)
        if step == 0:
            own_blocks, other_blocks, _ = lax.optimization_barrier(
                (coupling[0], other_coupling, low)
            )
            high_coupled = jnp.where(
                is_low,
                weighted(other_blocks, other_weights),
                weighted(own_blocks, weights),
            )
            low_coupled = jnp.where(
                is_low,
                weighted(own_blocks, weights),
                weighted(other_blocks, other_weights),
            )
        elif step == 1:
            high_map, low_map, _ = lax.optimization_barrier(
                (high_coupled, low_coupled, low)
            )
            parts = (
                jnp.dot(high_rows, high_inv, preferred_element_type=jnp.float32),
                composed(high_map, high_inv),
                jnp.dot(low_rows, low_inv, preferred_element_type=jnp.float32),
                composed(low_map, low_inv),
            )
        taken = chip == sender - 1
        nearer = jnp.where(taken, packed[:half], nearer)
        farther = jnp.where(taken, packed[half:], farther)
    low, high = composed_panels(nearer, farther, parts)

    back = swapped(jnp.where(is_low, high, low), "core")
    own = jnp.where(is_low, low, high)
    adjoint = jnp.where(
        side == 0,
        jnp.concatenate([own, back], axis=0),
        jnp.concatenate([back, own], axis=0),
    )

    high_fwd = jnp.where(is_low, other_fwd, mine_fwd)
    low_fwd = jnp.where(is_low, mine_fwd, other_fwd)
    partial_image = jnp.concatenate(
        [
            jnp.sum(low_fwd.astype(jnp.float32) * low.astype(jnp.float32), axis=0),
            jnp.sum(high_fwd.astype(jnp.float32) * high.astype(jnp.float32), axis=0),
        ]
    )
    grad = summed_over(partial_image, ("core", "src"))
    squares = summed_over(jnp.sum(grad * grad), ("chip",))
    count = float(chips * 2 * width)
    scale = jnp.sqrt(squares / count + 1e-06)
    direction = jnp.where(is_low, grad[:width], grad[width:]) / scale
    return (adjoint, direction)


def solution(mesh):
    chain = mesh.shape["chain"]
    src = mesh.shape["src"]
    devices = mesh.devices
    if mesh.axis_names != ("chain", "src"):
        devices = devices.T
    split = Mesh(devices.reshape(chain // 2, 2, src), ("chip", "core", "src"))
    return jax.shard_map(
        per_device,
        mesh=split,
        in_specs=(
            P("src", CHAIN),
            P("src", CHAIN),
            P(CHAIN, None, None),
            P(CHAIN, None, None, None),
            P(CHAIN, None),
        ),
        out_specs=(P("src", CHAIN), P(CHAIN)),
        check_vma=False,
    )
```

```python
import jax
import jax.numpy as jnp
from jax import lax
from jax.sharding import Mesh
from jax.sharding import PartitionSpec as P

CHAIN = ("chip", "core")


def shifted(x, axis, by):
    devices = lax.axis_size(axis)
    pairs = [(i, i + by) for i in range(devices) if 0 <= i + by < devices]
    return lax.ppermute(x, axis, pairs)


def swapped(x, axis):
    return lax.ppermute(x, axis, [(0, 1), (1, 0)])


def summed_over(x, axes):
    members = 1
    for axis in axes:
        members *= lax.axis_size(axis)
    spread = jnp.broadcast_to(x, (members,) + x.shape)
    return jnp.sum(lax.all_to_all(spread, axes, 0, 0, tiled=True), axis=0)


def solve_panel(rows, nearer, farther, inv_block, coupled):
    both = jnp.concatenate([nearer, farther], axis=1)
    total = rows.astype(jnp.float32) - jnp.dot(
        both, coupled, preferred_element_type=jnp.float32
    )
    return jnp.dot(
        total.astype(jnp.bfloat16), inv_block, preferred_element_type=jnp.float32
    ).astype(jnp.bfloat16)


def per_device(sources, forward, inv_diag, coupling, pattern):
    chips = lax.axis_size("chip")
    core = lax.axis_index("core")
    is_low = core == 0
    side = (core + lax.axis_index("chip")) % 2
    src_rows = sources.shape[0]
    half = src_rows // 2
    width = sources.shape[1]

    inv_block = inv_diag[0]
    weights = pattern[0].astype(coupling.dtype)
    weight_row = jnp.zeros((1, width), coupling.dtype).at[0, :2].set(weights)

    mine = lax.dynamic_slice_in_dim(sources, side * half, half, axis=0)
    mine_fwd = lax.dynamic_slice_in_dim(forward, side * half, half, axis=0)
    given = jnp.concatenate(
        [
            lax.dynamic_slice_in_dim(sources, (1 - side) * half, half, axis=0),
            lax.dynamic_slice_in_dim(forward, (1 - side) * half, half, axis=0),
            weight_row,
        ],
        axis=0,
    )
    other_coupling, other_inv, other_given = swapped(
        (coupling[0], inv_block, given), "core"
    )
    other_rows = other_given[:half]
    other_fwd = other_given[half : 2 * half]
    other_weights = other_given[2 * half, :2]

    def weighted(blocks, w):
        return jnp.concatenate([blocks[0] * w[0], blocks[1] * w[1]], axis=0)

    first_low = jnp.where(
        is_low, coupling[0, 0] * weights[0], other_coupling[0] * other_weights[0]
    )
    high_rows = jnp.where(is_low, other_rows, mine)
    low_rows = jnp.where(is_low, mine, other_rows)

    def by_inverse(rows, is_other):
        mixed = jnp.dot(rows, other_inv, preferred_element_type=jnp.float32)
        plain = jnp.dot(rows, inv_block, preferred_element_type=jnp.float32)
        return jnp.where(is_other, mixed, plain)

    def both_panels(nearer, farther):
        high = solve_panel(high_rows, nearer, farther, high_inv, high_coupled)
        low = solve_panel(low_rows, high, nearer, low_inv, low_coupled)
        return low, high

    def composed(coupled, inv):
        product = jnp.dot(coupled, inv, preferred_element_type=jnp.float32)
        return product.astype(jnp.bfloat16)

    def composed_panels(nearer, farther, parts):
        high_shift, high_map, low_shift, low_map = parts
        both = jnp.concatenate([nearer, farther], axis=1)
        high = (high_shift - jnp.dot(both, high_map, preferred_element_type=jnp.float32)).astype(jnp.bfloat16)
        both = jnp.concatenate([high, nearer], axis=1)
        low = (low_shift - jnp.dot(both, low_map, preferred_element_type=jnp.float32)).astype(jnp.bfloat16)
        return low, high

    chip = lax.axis_index("chip")
    nearer = jnp.zeros((half, width), jnp.bfloat16)
    farther = nearer
    parts = None
    for step in range(chips - 1):
        if parts is None:
            high = by_inverse(high_rows, is_low).astype(jnp.bfloat16)
            total = low_rows.astype(jnp.float32) - jnp.dot(
                high, first_low, preferred_element_type=jnp.float32
            )
            low = by_inverse(total.astype(jnp.bfloat16), ~is_low).astype(jnp.bfloat16)
        else:
            low, high = composed_panels(nearer, farther, parts)
        sender = chips - 1 - step
        pairs = [(2 * sender + c, 2 * (sender - 1) + 1 - c) for c in range(2)]
        packed = lax.ppermute(jnp.concatenate([low, high], axis=0), CHAIN, pairs)
        if parts is None:
            own_blocks, other_blocks, own_inv, later_inv, _ = lax.optimization_barrier(
                (coupling[0], other_coupling, inv_block, other_inv, low)
            )
            high_inv = jnp.where(is_low, later_inv, own_inv)
            low_inv = jnp.where(is_low, own_inv, later_inv)
            high_coupled = jnp.where(
                is_low,
                weighted(other_blocks, other_weights),
                weighted(own_blocks, weights),
            )
            low_coupled = jnp.where(
                is_low,
                weighted(own_blocks, weights),
                weighted(other_blocks, other_weights),
            )
            parts = (
                jnp.dot(high_rows, high_inv, preferred_element_type=jnp.float32),
                composed(high_coupled, high_inv),
                jnp.dot(low_rows, low_inv, preferred_element_type=jnp.float32),
                composed(low_coupled, low_inv),
            )
        taken = chip == sender - 1
        nearer = jnp.where(taken, packed[:half], nearer)
        farther = jnp.where(taken, packed[half:], farther)
    low, high = composed_panels(nearer, farther, parts)

    back = swapped(jnp.where(is_low, high, low), "core")
    own = jnp.where(is_low, low, high)
    adjoint = jnp.where(
        side == 0,
        jnp.concatenate([own, back], axis=0),
        jnp.concatenate([back, own], axis=0),
    )

    high_fwd = jnp.where(is_low, other_fwd, mine_fwd)
    low_fwd = jnp.where(is_low, mine_fwd, other_fwd)
    partial_image = jnp.concatenate(
        [
            jnp.sum(low_fwd.astype(jnp.float32) * low.astype(jnp.float32), axis=0),
            jnp.sum(high_fwd.astype(jnp.float32) * high.astype(jnp.float32), axis=0),
        ]
    )
    grad = summed_over(partial_image, ("core", "src"))
    squares = summed_over(jnp.sum(grad * grad), ("chip",))
    count = float(chips * 2 * width)
    scale = jnp.sqrt(squares / count + 1e-06)
    direction = jnp.where(is_low, grad[:width], grad[width:]) / scale
    return (adjoint, direction)


def solution(mesh):
    chain = mesh.shape["chain"]
    src = mesh.shape["src"]
    devices = mesh.devices
    if mesh.axis_names != ("chain", "src"):
        devices = devices.T
    split = Mesh(devices.reshape(chain // 2, 2, src), ("chip", "core", "src"))
    return jax.shard_map(
        per_device,
        mesh=split,
        in_specs=(
            P("src", CHAIN),
            P("src", CHAIN),
            P(CHAIN, None, None),
            P(CHAIN, None, None, None),
            P(CHAIN, None),
        ),
        out_specs=(P("src", CHAIN), P(CHAIN)),
        check_vma=False,
    )
```

```python
import jax
import jax.numpy as jnp
from jax import lax
from jax.sharding import Mesh
from jax.sharding import PartitionSpec as P

CHAIN = ("chip", "core")


def shifted(x, axis, by):
    devices = lax.axis_size(axis)
    pairs = [(i, i + by) for i in range(devices) if 0 <= i + by < devices]
    return lax.ppermute(x, axis, pairs)


def swapped(x, axis):
    return lax.ppermute(x, axis, [(0, 1), (1, 0)])


def summed_over(x, axes):
    members = 1
    for axis in axes:
        members *= lax.axis_size(axis)
    spread = jnp.broadcast_to(x, (members,) + x.shape)
    return jnp.sum(lax.all_to_all(spread, axes, 0, 0, tiled=True), axis=0)


def solve_panel(rows, nearer, farther, inv_block, coupled):
    both = jnp.concatenate([nearer, farther], axis=1)
    total = rows.astype(jnp.float32) - jnp.dot(
        both, coupled, preferred_element_type=jnp.float32
    )
    return jnp.dot(
        total.astype(jnp.bfloat16), inv_block, preferred_element_type=jnp.float32
    ).astype(jnp.bfloat16)


def per_device(sources, forward, inv_diag, coupling, pattern):
    chips = lax.axis_size("chip")
    core = lax.axis_index("core")
    is_low = core == 0
    side = (core + lax.axis_index("chip")) % 2
    src_rows = sources.shape[0]
    half = src_rows // 2
    width = sources.shape[1]

    inv_block = inv_diag[0]
    weights = pattern[0].astype(coupling.dtype)
    weight_row = jnp.zeros((1, width), coupling.dtype).at[0, :2].set(weights)

    mine = lax.dynamic_slice_in_dim(sources, side * half, half, axis=0)
    mine_fwd = lax.dynamic_slice_in_dim(forward, side * half, half, axis=0)
    given = jnp.concatenate(
        [
            lax.dynamic_slice_in_dim(sources, (1 - side) * half, half, axis=0),
            lax.dynamic_slice_in_dim(forward, (1 - side) * half, half, axis=0),
            weight_row,
        ],
        axis=0,
    )
    other_first, other_inv, other_given = swapped(
        (coupling[0, 0], inv_block, given), "core"
    )
    other_rows = other_given[:half]
    other_fwd = other_given[half : 2 * half]
    other_weights = other_given[2 * half, :2]

    def weighted(blocks, w):
        return jnp.concatenate([blocks[0] * w[0], blocks[1] * w[1]], axis=0)

    first_low = jnp.where(
        is_low, coupling[0, 0] * weights[0], other_first * other_weights[0]
    )
    high_inv = jnp.where(is_low, other_inv, inv_block)
    high_rows = jnp.where(is_low, other_rows, mine)
    low_inv = jnp.where(is_low, inv_block, other_inv)
    low_rows = jnp.where(is_low, mine, other_rows)

    def both_panels(nearer, farther):
        high = solve_panel(high_rows, nearer, farther, high_inv, high_coupled)
        low = solve_panel(low_rows, high, nearer, low_inv, low_coupled)
        return low, high

    def composed(coupled, inv):
        product = jnp.dot(coupled, inv, preferred_element_type=jnp.float32)
        return product.astype(jnp.bfloat16)

    def composed_panels(nearer, farther, parts):
        high_shift, high_map, low_shift, low_map = parts
        both = jnp.concatenate([nearer, farther], axis=1)
        high = (high_shift - jnp.dot(both, high_map, preferred_element_type=jnp.float32)).astype(jnp.bfloat16)
        both = jnp.concatenate([high, nearer], axis=1)
        low = (low_shift - jnp.dot(both, low_map, preferred_element_type=jnp.float32)).astype(jnp.bfloat16)
        return low, high

    chip = lax.axis_index("chip")
    nearer = jnp.zeros((half, width), jnp.bfloat16)
    farther = nearer
    parts = None
    for step in range(chips - 1):
        if parts is None:
            high = jnp.dot(
                high_rows, high_inv, preferred_element_type=jnp.float32
            ).astype(jnp.bfloat16)
            total = low_rows.astype(jnp.float32) - jnp.dot(
                high, first_low, preferred_element_type=jnp.float32
            )
            low = jnp.dot(
                total.astype(jnp.bfloat16), low_inv, preferred_element_type=jnp.float32
            ).astype(jnp.bfloat16)
        else:
            low, high = composed_panels(nearer, farther, parts)
        sender = chips - 1 - step
        pairs = [(2 * sender + c, 2 * (sender - 1) + 1 - c) for c in range(2)]
        packed = lax.ppermute(jnp.concatenate([low, high], axis=0), CHAIN, pairs)
        if parts is None:
            second, _ = lax.optimization_barrier((coupling[0, 1], low))
            other_second = swapped(second, "core")
            own_blocks = (coupling[0, 0], coupling[0, 1])
            other_blocks = (other_first, other_second)
            high_coupled = jnp.where(
                is_low,
                weighted(other_blocks, other_weights),
                weighted(own_blocks, weights),
            )
            low_coupled = jnp.where(
                is_low,
                weighted(own_blocks, weights),
                weighted(other_blocks, other_weights),
            )
            parts = (
                jnp.dot(high_rows, high_inv, preferred_element_type=jnp.float32),
                composed(high_coupled, high_inv),
                jnp.dot(low_rows, low_inv, preferred_element_type=jnp.float32),
                composed(low_coupled, low_inv),
            )
        taken = chip == sender - 1
        nearer = jnp.where(taken, packed[:half], nearer)
        farther = jnp.where(taken, packed[half:], farther)
    low, high = composed_panels(nearer, farther, parts)

    back = swapped(jnp.where(is_low, high, low), "core")
    own = jnp.where(is_low, low, high)
    adjoint = jnp.where(
        side == 0,
        jnp.concatenate([own, back], axis=0),
        jnp.concatenate([back, own], axis=0),
    )

    high_fwd = jnp.where(is_low, other_fwd, mine_fwd)
    low_fwd = jnp.where(is_low, mine_fwd, other_fwd)
    partial_image = jnp.concatenate(
        [
            jnp.sum(low_fwd.astype(jnp.float32) * low.astype(jnp.float32), axis=0),
            jnp.sum(high_fwd.astype(jnp.float32) * high.astype(jnp.float32), axis=0),
        ]
    )
    grad = summed_over(partial_image, ("core", "src"))
    squares = summed_over(jnp.sum(grad * grad), ("chip",))
    count = float(chips * 2 * width)
    scale = jnp.sqrt(squares / count + 1e-06)
    direction = jnp.where(is_low, grad[:width], grad[width:]) / scale
    return (adjoint, direction)


def solution(mesh):
    chain = mesh.shape["chain"]
    src = mesh.shape["src"]
    devices = mesh.devices
    if mesh.axis_names != ("chain", "src"):
        devices = devices.T
    split = Mesh(devices.reshape(chain // 2, 2, src), ("chip", "core", "src"))
    return jax.shard_map(
        per_device,
        mesh=split,
        in_specs=(
            P("src", CHAIN),
            P("src", CHAIN),
            P(CHAIN, None, None),
            P(CHAIN, None, None, None),
            P(CHAIN, None),
        ),
        out_specs=(P("src", CHAIN), P(CHAIN)),
        check_vma=False,
    )
```
